32 devices in a mesh: ctx: 16 (over z, y, x), dp: 2 (over core).
Axes of the slice: x: 2, y: 2, z: 4, core: 2. Of those that a mesh axis runs over, the one named last changes fastest.
Arguments:
- queries: bfloat16 [2, 16, 2, 64, 4096], P('dp', 'ctx'), may hold values from -12 to 12
- keys: bfloat16 [2, 16, 2, 64, 512], P('dp', 'ctx'), may hold values from -12 to 12
- values: bfloat16 [2, 16, 2, 64, 512], P('dp', 'ctx'), may hold values from -6 to 6
- doc_bounds: int32 [2, 16, 2, 2, 64], P('dp', 'ctx'), may hold values from 0 to 2047, as said below
- sink_logit: float32 [32], replicated, may hold values from 0 to 3
- out_grad: bfloat16 [2, 16, 2, 64, 4096], P('dp', 'ctx'), may hold values from -9 to 9
Outputs:
- attn_out: bfloat16 [2, 16, 2, 64, 4096], P('dp', 'ctx')
- query_grad: bfloat16 [2, 16, 2, 64, 4096], P('dp', 'ctx')
- key_grad: bfloat16 [2, 16, 2, 64, 512], P('dp', 'ctx')
- value_grad: bfloat16 [2, 16, 2, 64, 512], P('dp', 'ctx')
- sink_grad: float32 [32], replicated
The draws below stay inside these ranges and needn't reach their ends.
Inputs may be any that keep to these rules, and one draw needn't show every extreme that they name: `doc_bounds`: documents are contiguous runs that tile each pack in position order, each of 1 to 64 tokens; every pack has one of exactly 64 tokens; both entries of a token name its own document's first and last position.
All inputs are finite; a program needn't handle non-finite values.
Results may differ from the reference program's by a relative error of at most 0.025.
Values may be sent and summed in bfloat16 or wider, within the bound.
No kernel may reach another device: no remote copies, remote signals or barrier semaphores. Data moves between devices by JAX's collectives and lax.ppermute only.
A program may use at most 64 MiB of HBM per device.

```python
import math
import jax
import jax.numpy as jnp
from jax import lax

HEADS = 32
KV_HEADS = 4
HEAD_DIM = 128
GROUP = 8
BLOCK = 64
REACH = 1
PAIRS = 16
PACKS = 2
LENGTH = 2048
DOC_MOST = 64


def to_paired_drawn(array_in):
    shaped = array_in.reshape((PACKS, 2 * PAIRS, BLOCK) + array_in.shape[2:])
    first = shaped[:, :PAIRS]
    second = jnp.flip(shaped[:, PAIRS:], axis=1)
    return jnp.stack([first, second], axis=2)


def pack_bounds(pack_key):
    length_key, chosen_key = jax.random.split(pack_key)
    lengths = jax.random.randint(length_key, (LENGTH,), 1, DOC_MOST + 1, dtype=jnp.int32)
    chosen = jax.random.randint(chosen_key, (), 0, 8, dtype=jnp.int32)
    places = jnp.arange(LENGTH, dtype=jnp.int32)
    lengths = jnp.where(places == chosen, DOC_MOST, lengths)
    ends = jnp.cumsum(lengths).astype(jnp.int32)
    doc_index = jnp.searchsorted(ends, places, side='right')
    starts = ends - lengths
    first_pos = starts[doc_index]
    last_pos = jnp.minimum(ends[doc_index], LENGTH) - 1
    return (first_pos.astype(jnp.int32), last_pos.astype(jnp.int32))


def natural_bounds(key):
    pack_keys = jax.random.split(jax.random.fold_in(key, 11), PACKS)
    return jax.vmap(pack_bounds)(pack_keys)


def draw_doc_bounds(key, part):
    first_pos, last_pos = natural_bounds(key)
    return jnp.stack([to_paired_drawn(first_pos), to_paired_drawn(last_pos)], axis=3)


def draw_queries(key, part):
    base_key = jax.random.fold_in(key, 31)
    full_shape = (PACKS, LENGTH, HEADS * HEAD_DIM)
    base = jax.random.truncated_normal(base_key, -6.0, 6.0, full_shape)
    return to_paired_drawn(base).astype(jnp.bfloat16)


def draw_keys(key, part):
    base_key = jax.random.fold_in(key, 32)
    full_shape = (PACKS, LENGTH, KV_HEADS, HEAD_DIM)
    base = jax.random.truncated_normal(base_key, -6.0, 6.0, full_shape)
    return to_paired_drawn(base.reshape(PACKS, LENGTH, KV_HEADS * HEAD_DIM)).astype(jnp.bfloat16)


def draw_out_grad(key, part):
    base_key = jax.random.fold_in(key, 33)
    full_shape = (PACKS, LENGTH, HEADS * HEAD_DIM)
    ramp = jnp.arange(PAIRS, dtype=jnp.float32) / (PAIRS - 1)
    base = jax.random.truncated_normal(base_key, -6.0, 6.0, full_shape)
    rising = 0.5 + ramp
    paired = to_paired_drawn(base)
    return (paired * rising[None, :, None, None, None]).astype(jnp.bfloat16)


def block_levels(rng, extent, cuts, smallest, high):
    level = 1.0
    for position, parts in cuts:
        steps = jax.random.uniform(jax.random.fold_in(jax.random.fold_in(rng, 6), position), (parts,), jnp.float32, smallest / len(cuts), high / len(cuts))
        level = level * jnp.repeat(jnp.exp(steps), extent[position] // parts).reshape((-1,) + (1,) * (len(extent) - 1 - position))
    return level


def normal_values(own_key, shape, scale, limit, shards=(), held_as=jnp.bfloat16):
    loudness = block_levels(own_key, shape, shards, -0.22, 0.18) if shards else 1.0
    entries = jax.random.normal(own_key, shape, jnp.float32) * scale * loudness
    return jnp.minimum(jnp.maximum(entries, -limit), limit).astype(held_as)


def setup_inputs(seed: int = 0) -> dict:
    splits = jax.random.split(jax.random.key(seed), 7)
    return {
        "queries": draw_queries(jax.random.fold_in(splits[6], 71), 0),
        "keys": draw_keys(jax.random.fold_in(splits[6], 71), 0),
        "values": normal_values(splits[2], (PACKS, PAIRS, 2, BLOCK, KV_HEADS * HEAD_DIM), 1.0, 6.0, ((0, 2), (1, 16))),
        "doc_bounds": draw_doc_bounds(jax.random.fold_in(splits[6], 71), 0),
        "sink_logit": jnp.clip(jax.random.uniform(splits[4], (HEADS,), jnp.float32, 0.0, 3.0), 0.0, 3.0),
        "out_grad": draw_out_grad(jax.random.fold_in(splits[6], 71), 0),
    }


def to_natural(array_in):
    first = array_in[:, :, 0]
    second = jnp.flip(array_in[:, :, 1], axis=1)
    return jnp.concatenate([first, second], axis=1)

def to_paired(array_in):
    half = array_in.shape[1] // 2
    first = array_in[:, :half]
    second = jnp.flip(array_in[:, half:], axis=1)
    return jnp.stack([first, second], axis=2)

def pack_pass(query_pack, key_pack, value_pack, bound_pack, grad_pack, sink_logit):
    block_count = query_pack.shape[0]
    span = (REACH + 1) * BLOCK
    score_scale = 1.0 / math.sqrt(HEAD_DIM)
    blank = jnp.zeros((REACH, BLOCK, KV_HEADS * HEAD_DIM), key_pack.dtype)
    keys_wide = jnp.concatenate([blank, key_pack], axis=0)
    values_wide = jnp.concatenate([blank, value_pack], axis=0)
    sink_col = sink_logit.reshape(KV_HEADS, GROUP, 1)
    row_offsets = jnp.arange(BLOCK, dtype=jnp.int32)
    window_offsets = jnp.arange(span, dtype=jnp.int32)

    def one_block(block_index):
        block_index = block_index.astype(jnp.int32)
        grouped = query_pack[block_index].reshape(BLOCK, KV_HEADS, GROUP, HEAD_DIM).astype(jnp.float32)
        grad_rows = grad_pack[block_index].reshape(BLOCK, KV_HEADS, GROUP, HEAD_DIM).astype(jnp.float32)
        key_rows = lax.dynamic_slice_in_dim(keys_wide, block_index, REACH + 1, 0)
        key_rows = key_rows.reshape(span, KV_HEADS, HEAD_DIM).astype(jnp.float32)
        value_rows = lax.dynamic_slice_in_dim(values_wide, block_index, REACH + 1, 0)
        value_rows = value_rows.reshape(span, KV_HEADS, HEAD_DIM).astype(jnp.float32)
        query_pos = block_index * BLOCK + row_offsets
        key_pos = (block_index - REACH) * BLOCK + window_offsets
        first_pos = bound_pack[block_index, 0]
        allowed = (key_pos[None, :] <= query_pos[:, None]) & (key_pos[None, :] >= first_pos[:, None])
        scores = jnp.einsum('tkgd,ukd->kgtu', grouped, key_rows) * score_scale
        masked = jnp.where(allowed[None, None], scores, -jnp.inf)
        row_top = jnp.maximum(lax.optimization_barrier(jnp.max(masked, axis=-1)), sink_col)
        row_total = jnp.exp(sink_col - row_top) + lax.optimization_barrier(jnp.sum(jnp.exp(masked - row_top[..., None]), axis=-1))
        log_total = row_top + jnp.log(row_total)
        weights32 = jnp.exp(masked - log_total[..., None])
        weights = weights32.astype(jnp.bfloat16)
        attended = jnp.einsum('kgtu,ukd->tkgd', weights.astype(jnp.float32), value_rows).astype(jnp.bfloat16)
        row_delta = lax.optimization_barrier(jnp.sum(grad_rows * attended.astype(jnp.float32), axis=-1))
        delta_cols = jnp.transpose(row_delta, (1, 2, 0))
        dprob = jnp.einsum('tkgd,ukd->kgtu', grad_rows, value_rows)
        dscore = (weights32 * (dprob - delta_cols[..., None])).astype(jnp.bfloat16)
        dquery = jnp.einsum('kgtu,ukd->tkgd', dscore.astype(jnp.float32), key_rows) * score_scale
        dkey = jnp.einsum('kgtu,tkgd->ukd', dscore.astype(jnp.float32), grouped) * score_scale
        dvalue = jnp.einsum('kgtu,tkgd->ukd', weights.astype(jnp.float32), grad_rows)
        sink_part = -lax.optimization_barrier(jnp.sum(jnp.exp(sink_col - log_total) * delta_cols, axis=-1))
        return (attended.reshape(BLOCK, HEADS * HEAD_DIM), dquery.astype(jnp.bfloat16).reshape(BLOCK, HEADS * HEAD_DIM), dkey.reshape(REACH + 1, BLOCK, KV_HEADS * HEAD_DIM), dvalue.reshape(REACH + 1, BLOCK, KV_HEADS * HEAD_DIM), sink_part.reshape(HEADS))
    attended, dquery, dkey, dvalue, sink_parts = lax.map(one_block, jnp.arange(block_count, dtype=jnp.int32))
    tail = jnp.zeros((REACH, REACH + 1, BLOCK, KV_HEADS * HEAD_DIM), jnp.float32)
    dkey = jnp.concatenate([dkey, tail], axis=0)
    dvalue = jnp.concatenate([dvalue, tail], axis=0)
    key_total = jnp.zeros((block_count, BLOCK, KV_HEADS * HEAD_DIM), jnp.float32)
    value_total = jnp.zeros((block_count, BLOCK, KV_HEADS * HEAD_DIM), jnp.float32)
    for window_slot in range(REACH + 1):
        lead = REACH - window_slot
        key_total = key_total + dkey[lead:lead + block_count, window_slot]
        value_total = value_total + dvalue[lead:lead + block_count, window_slot]
    return (attended, dquery, key_total.astype(jnp.bfloat16), value_total.astype(jnp.bfloat16), lax.optimization_barrier(jnp.sum(sink_parts, axis=0)))

def reference(queries, keys, values, doc_bounds, sink_logit, out_grad):
    packed = (to_natural(queries), to_natural(keys), to_natural(values), to_natural(doc_bounds), to_natural(out_grad))

    def per_pack(items):
        return pack_pass(items[0], items[1], items[2], items[3], items[4], sink_logit)
    attended, dquery, key_total, value_total, sink_parts = lax.map(per_pack, packed)
    sink_grad = lax.optimization_barrier(jnp.sum(sink_parts, axis=0))
    return (to_paired(attended), to_paired(dquery), to_paired(key_total), to_paired(value_total), sink_grad)
```

```python
import math

import jax
import jax.numpy as jnp
from jax import lax
from jax.sharding import PartitionSpec as P

HEADS = 32
KV_HEADS = 4
HEAD_DIM = 128
GROUP = 8
REACH = 1


def shift_up(x, axis):
    size = lax.axis_size(axis)
    return lax.ppermute(x, axis, [(i, i + 1) for i in range(size - 1)])


def shift_down(x, axis):
    size = lax.axis_size(axis)
    return lax.ppermute(x, axis, [(i + 1, i) for i in range(size - 1)])


def all_sum(x, axes):
    for axis in axes:
        size = lax.axis_size(axis)
        if size & (size - 1):
            x = lax.psum(x, axis)
            continue
        bit = 1
        while bit < size:
            x = x + lax.ppermute(x, axis, [(i, i ^ bit) for i in range(size)])
            bit *= 2
    return x


def per_device(queries, keys, values, doc_bounds, sink_logit, out_grad):
    block_rows = queries.shape[3]
    query_width = queries.shape[4]
    value_width = keys.shape[4]
    pair_count = lax.axis_size("ctx")
    my_index = lax.axis_index("ctx")
    score_scale = 1.0 / math.sqrt(HEAD_DIM)
    at_fold = my_index == pair_count - 1
    last_block = 2 * pair_count - 1
    span = (REACH + 1) * block_rows

    query_lanes = queries.reshape(2, block_rows, KV_HEADS, GROUP, HEAD_DIM)
    grad_lanes = out_grad.reshape(2, block_rows, KV_HEADS, GROUP, HEAD_DIM)
    own_pair = jnp.concatenate(
        [keys.reshape(2, block_rows, value_width), values.reshape(2, block_rows, value_width)], axis=2
    )
    prev0 = shift_up(own_pair[0], "ctx")
    prev1 = shift_down(own_pair[1], "ctx")
    prev1 = jnp.where(at_fold, own_pair[0], prev1)
    prev_pair = jnp.stack([prev0, prev1])
    window = jnp.concatenate([prev_pair, own_pair], axis=1)
    window_keys = window[:, :, :value_width].reshape(2, span, KV_HEADS, HEAD_DIM)
    window_values = window[:, :, value_width:].reshape(2, span, KV_HEADS, HEAD_DIM)

    lane_block = jnp.stack([my_index, last_block - my_index]).astype(jnp.int32)
    row_offsets = jnp.arange(block_rows, dtype=jnp.int32)
    window_offsets = jnp.arange(span, dtype=jnp.int32)
    query_pos = lane_block[:, None] * block_rows + row_offsets[None, :]
    key_pos = (lane_block[:, None] - REACH) * block_rows + window_offsets[None, :]
    first_pos = doc_bounds.reshape(2, 2, block_rows)[:, 0]
    allowed = (key_pos[:, None, :] <= query_pos[:, :, None]) & (
        key_pos[:, None, :] >= first_pos[:, :, None]
    )
    allowed = allowed[:, None, None]
    sink_col = sink_logit.reshape(1, KV_HEADS, GROUP, 1)

    scores = (
        jnp.einsum(
            "ltkgd,lukd->lkgtu", query_lanes, window_keys, preferred_element_type=jnp.float32
        )
        * score_scale
    )
    masked = jnp.where(allowed, scores, -jnp.inf)
    row_top = jnp.maximum(sink_col, jnp.max(masked, axis=-1))
    row_total = jnp.exp(sink_col - row_top) + jnp.sum(jnp.exp(masked - row_top[..., None]), axis=-1)
    log_total = row_top + jnp.log(row_total)
    probs = jnp.exp(masked - log_total[..., None])
    weights = probs.astype(jnp.bfloat16)
    attended = jnp.einsum(
        "lkgtu,lukd->ltkgd", weights, window_values, preferred_element_type=jnp.float32
    ).astype(jnp.bfloat16)
    row_delta = jnp.sum(grad_lanes.astype(jnp.float32) * attended.astype(jnp.float32), axis=-1)
    delta_cols = jnp.transpose(row_delta, (0, 2, 3, 1))
    sink_terms = -jnp.sum(jnp.exp(sink_col - log_total) * delta_cols, axis=(0, 3))
    sink_grad = all_sum(sink_terms.reshape(HEADS), ("dp", "ctx"))

    dprob = jnp.einsum(
        "ltkgd,lukd->lkgtu", grad_lanes, window_values, preferred_element_type=jnp.float32
    )
    dscore = (probs * (dprob - delta_cols[..., None])).astype(jnp.bfloat16)
    key_part = (
        jnp.einsum("lkgtu,ltkgd->lukd", dscore, query_lanes, preferred_element_type=jnp.float32)
        * score_scale
    )
    value_part = jnp.einsum(
        "lkgtu,ltkgd->lukd", weights, grad_lanes, preferred_element_type=jnp.float32
    )
    partial = jnp.concatenate(
        [key_part.reshape(2, span, value_width), value_part.reshape(2, span, value_width)], axis=2
    )
    dquery = (
        jnp.einsum("lkgtu,lukd->ltkgd", dscore, window_keys, preferred_element_type=jnp.float32)
        * score_scale
    )

    prev_part = partial[:, :block_rows].astype(jnp.bfloat16)
    into0 = shift_down(prev_part[0], "ctx")
    into1 = shift_up(prev_part[1], "ctx")
    into0 = jnp.where(at_fold, prev_part[1], into0)
    own_part = partial[:, block_rows:]
    gathered = own_part + jnp.stack([into0, into1]).astype(jnp.float32)

    out_shape = (1, 1, 2, block_rows, query_width)
    pair_out = (1, 1, 2, block_rows, value_width)
    attn_out = attended.reshape(out_shape)
    query_grad = dquery.astype(jnp.bfloat16).reshape(out_shape)
    key_grad = gathered[:, :, :value_width].astype(jnp.bfloat16).reshape(pair_out)
    value_grad = gathered[:, :, value_width:].astype(jnp.bfloat16).reshape(pair_out)
    return (attn_out, query_grad, key_grad, value_grad, sink_grad)


def solution(mesh):
    in_specs = (
        P("dp", "ctx", None, None, None),
        P("dp", "ctx", None, None, None),
        P("dp", "ctx", None, None, None),
        P("dp", "ctx", None, None, None),
        P(),
        P("dp", "ctx", None, None, None),
    )
    out_specs = (
        P("dp", "ctx", None, None, None),
        P("dp", "ctx", None, None, None),
        P("dp", "ctx", None, None, None),
        P("dp", "ctx", None, None, None),
        P(),
    )
    return jax.shard_map(
        per_device, mesh=mesh, in_specs=in_specs, out_specs=out_specs, check_vma=False
    )
```

```python
import math

import jax
import jax.numpy as jnp
from jax import lax
from jax.sharding import PartitionSpec as P

HEADS = 32
KV_HEADS = 4
HEAD_DIM = 128
GROUP = 8
REACH = 1


def shift_up(x, axis):
    size = lax.axis_size(axis)
    return lax.ppermute(x, axis, [(i, i + 1) for i in range(size - 1)])


def shift_down(x, axis):
    size = lax.axis_size(axis)
    return lax.ppermute(x, axis, [(i + 1, i) for i in range(size - 1)])


def all_sum(x, axes):
    count = 1
    for axis in axes:
        count *= lax.axis_size(axis)
    spread = jnp.broadcast_to(x[None], (count,) + x.shape)
    return jnp.sum(lax.all_to_all(spread, axes, 0, 0, tiled=True), axis=0)


def per_device(queries, keys, values, doc_bounds, sink_logit, out_grad):
    block_rows = queries.shape[3]
    query_width = queries.shape[4]
    value_width = keys.shape[4]
    pair_count = lax.axis_size("ctx")
    my_index = lax.axis_index("ctx")
    score_scale = 1.0 / math.sqrt(HEAD_DIM)
    at_fold = my_index == pair_count - 1
    last_block = 2 * pair_count - 1
    span = (REACH + 1) * block_rows

    query_lanes = queries.reshape(2, block_rows, KV_HEADS, GROUP, HEAD_DIM)
    grad_lanes = out_grad.reshape(2, block_rows, KV_HEADS, GROUP, HEAD_DIM)
    own_pair = jnp.concatenate(
        [keys.reshape(2, block_rows, value_width), values.reshape(2, block_rows, value_width)], axis=2
    )
    send0, send1 = lax.optimization_barrier((own_pair[0], own_pair[1]))
    prev0 = shift_up(send0, "ctx")
    prev1 = shift_down(send1, "ctx")
    prev1 = jnp.where(at_fold, own_pair[0], prev1)
    prev_pair = jnp.stack([prev0, prev1])
    window = jnp.concatenate([prev_pair, own_pair], axis=1)
    window_keys = window[:, :, :value_width].reshape(2, span, KV_HEADS, HEAD_DIM)
    window_values = window[:, :, value_width:].reshape(2, span, KV_HEADS, HEAD_DIM)

    lane_block = jnp.stack([my_index, last_block - my_index]).astype(jnp.int32)
    row_offsets = jnp.arange(block_rows, dtype=jnp.int32)
    window_offsets = jnp.arange(span, dtype=jnp.int32)
    query_pos = lane_block[:, None] * block_rows + row_offsets[None, :]
    key_pos = (lane_block[:, None] - REACH) * block_rows + window_offsets[None, :]
    first_pos = doc_bounds.reshape(2, 2, block_rows)[:, 0]
    allowed = (key_pos[:, None, :] <= query_pos[:, :, None]) & (
        key_pos[:, None, :] >= first_pos[:, :, None]
    )
    allowed = allowed[:, None, None]
    sink_col = sink_logit.reshape(1, KV_HEADS, GROUP, 1)

    scores = (
        jnp.einsum(
            "ltkgd,lukd->lkgtu", query_lanes, window_keys, preferred_element_type=jnp.float32
        )
        * score_scale
    )
    masked = jnp.where(allowed, scores, -jnp.inf)
    row_top = jnp.maximum(sink_col, jnp.max(masked, axis=-1))
    row_total = jnp.exp(sink_col - row_top) + jnp.sum(jnp.exp(masked - row_top[..., None]), axis=-1)
    log_total = row_top + jnp.log(row_total)
    probs = jnp.exp(masked - log_total[..., None])
    weights = probs.astype(jnp.bfloat16)
    attended = jnp.einsum(
        "lkgtu,lukd->ltkgd", weights, window_values, preferred_element_type=jnp.float32
    ).astype(jnp.bfloat16)
    row_delta = jnp.sum(grad_lanes.astype(jnp.float32) * attended.astype(jnp.float32), axis=-1)
    delta_cols = jnp.transpose(row_delta, (0, 2, 3, 1))
    sink_terms = -jnp.sum(jnp.exp(sink_col - log_total) * delta_cols, axis=(0, 3))
    sink_grad = all_sum(sink_terms.reshape(HEADS), ("ctx", "dp"))

    dprob = jnp.einsum(
        "ltkgd,lukd->lkgtu", grad_lanes, window_values, preferred_element_type=jnp.float32
    )
    dscore = (probs * (dprob - delta_cols[..., None])).astype(jnp.bfloat16)
    key_part = (
        jnp.einsum("lkgtu,ltkgd->lukd", dscore, query_lanes, preferred_element_type=jnp.float32)
        * score_scale
    )
    value_part = jnp.einsum(
        "lkgtu,ltkgd->lukd", weights, grad_lanes, preferred_element_type=jnp.float32
    )
    partial = jnp.concatenate(
        [key_part.reshape(2, span, value_width), value_part.reshape(2, span, value_width)], axis=2
    )
    dquery = (
        jnp.einsum("lkgtu,lukd->ltkgd", dscore, window_keys, preferred_element_type=jnp.float32)
        * score_scale
    )

    prev_part = partial[:, :block_rows].astype(jnp.bfloat16)
    send0, send1 = lax.optimization_barrier((prev_part[0], prev_part[1]))
    into0 = shift_down(send0, "ctx")
    into1 = shift_up(send1, "ctx")
    into0 = jnp.where(at_fold, prev_part[1], into0)
    own_part = partial[:, block_rows:]
    gathered = own_part + jnp.stack([into0, into1]).astype(jnp.float32)

    out_shape = (1, 1, 2, block_rows, query_width)
    pair_out = (1, 1, 2, block_rows, value_width)
    attn_out = attended.reshape(out_shape)
    query_grad = dquery.astype(jnp.bfloat16).reshape(out_shape)
    key_grad = gathered[:, :, :value_width].astype(jnp.bfloat16).reshape(pair_out)
    value_grad = gathered[:, :, value_width:].astype(jnp.bfloat16).reshape(pair_out)
    return (attn_out, query_grad, key_grad, value_grad, sink_grad)


def solution(mesh):
    in_specs = (
        P("dp", "ctx", None, None, None),
        P("dp", "ctx", None, None, None),
        P("dp", "ctx", None, None, None),
        P("dp", "ctx", None, None, None),
        P(),
        P("dp", "ctx", None, None, None),
    )
    out_specs = (
        P("dp", "ctx", None, None, None),
        P("dp", "ctx", None, None, None),
        P("dp", "ctx", None, None, None),
        P("dp", "ctx", None, None, None),
        P(),
    )
    return jax.shard_map(
        per_device, mesh=mesh, in_specs=in_specs, out_specs=out_specs, check_vma=False
    )
```

```python
import math

import jax
import jax.numpy as jnp
from jax import lax
from jax.sharding import PartitionSpec as P

HEADS = 32
KV_HEADS = 4
HEAD_DIM = 128
GROUP = 8
REACH = 1


def shift_up(x, axis):
    size = lax.axis_size(axis)
    return lax.ppermute(x, axis, [(i, i + 1) for i in range(size - 1)])


def shift_down(x, axis):
    size = lax.axis_size(axis)
    return lax.ppermute(x, axis, [(i + 1, i) for i in range(size - 1)])


def all_sum(x, axes):
    count = 1
    for axis in axes:
        count *= lax.axis_size(axis)
    spread = jnp.broadcast_to(x[None], (count,) + x.shape)
    return jnp.sum(lax.all_to_all(spread, axes, 0, 0, tiled=True), axis=0)


def per_device(queries, keys, values, doc_bounds, sink_logit, out_grad):
    block_rows = queries.shape[3]
    query_width = queries.shape[4]
    value_width = keys.shape[4]
    pair_count = lax.axis_size("ctx")
    my_index = lax.axis_index("ctx")
    score_scale = 1.0 / math.sqrt(HEAD_DIM)
    at_fold = my_index == pair_count - 1
    last_block = 2 * pair_count - 1
    span = (REACH + 1) * block_rows

    query_lanes = queries.reshape(2, block_rows, KV_HEADS, GROUP, HEAD_DIM)
    grad_lanes = out_grad.reshape(2, block_rows, KV_HEADS, GROUP, HEAD_DIM)
    own_pair = jnp.concatenate(
        [keys.reshape(2, block_rows, value_width), values.reshape(2, block_rows, value_width)], axis=2
    )
    send0, send1 = lax.optimization_barrier((own_pair[0], own_pair[1]))
    prev0 = shift_up(send0, "ctx")
    prev1 = shift_down(send1, "ctx")
    prev1 = jnp.where(at_fold, own_pair[0], prev1)
    prev_pair = jnp.stack([prev0, prev1])
    own_keys = own_pair[:, :, :value_width].reshape(2, block_rows, KV_HEADS, HEAD_DIM)
    own_values = own_pair[:, :, value_width:].reshape(2, block_rows, KV_HEADS, HEAD_DIM)
    prev_keys = prev_pair[:, :, :value_width].reshape(2, block_rows, KV_HEADS, HEAD_DIM)
    prev_values = prev_pair[:, :, value_width:].reshape(2, block_rows, KV_HEADS, HEAD_DIM)

    lane_block = jnp.stack([my_index, last_block - my_index]).astype(jnp.int32)
    row_offsets = jnp.arange(block_rows, dtype=jnp.int32)
    query_pos = lane_block[:, None] * block_rows + row_offsets[None, :]
    prev_pos = query_pos - REACH * block_rows
    first_pos = doc_bounds.reshape(2, 2, block_rows)[:, 0]
    allowed_own = (query_pos[:, None, :] <= query_pos[:, :, None]) & (
        query_pos[:, None, :] >= first_pos[:, :, None]
    )
    allowed_prev = prev_pos[:, None, :] >= first_pos[:, :, None]
    allowed_own = allowed_own[:, None, None]
    allowed_prev = allowed_prev[:, None, None]
    sink_col = sink_logit.reshape(1, KV_HEADS, GROUP, 1)

    def block_scores(side_keys):
        return (
            jnp.einsum(
                "ltkgd,lukd->lkgtu", query_lanes, side_keys, preferred_element_type=jnp.float32
            )
            * score_scale
        )

    def grad_scores(side_values):
        return jnp.einsum(
            "ltkgd,lukd->lkgtu", grad_lanes, side_values, preferred_element_type=jnp.float32
        )

    def mix(side_weights, side_rows):
        return jnp.einsum(
            "lkgtu,lukd->ltkgd", side_weights, side_rows, preferred_element_type=jnp.float32
        )

    def key_side(side_weights, rows):
        summed = jnp.einsum(
            "lkgtu,ltkgd->lukd", side_weights, rows, preferred_element_type=jnp.float32
        )
        return summed.reshape(2, block_rows, value_width)

    masked_own = jnp.where(allowed_own, block_scores(own_keys), -jnp.inf)
    dprob_own = grad_scores(own_values)
    masked_prev = jnp.where(allowed_prev, block_scores(prev_keys), -jnp.inf)

    row_top = jnp.maximum(
        sink_col, jnp.maximum(jnp.max(masked_own, axis=-1), jnp.max(masked_prev, axis=-1))
    )
    row_total = (
        jnp.exp(sink_col - row_top)
        + jnp.sum(jnp.exp(masked_own - row_top[..., None]), axis=-1)
        + jnp.sum(jnp.exp(masked_prev - row_top[..., None]), axis=-1)
    )
    log_total = row_top + jnp.log(row_total)
    probs_own = jnp.exp(masked_own - log_total[..., None])
    probs_prev = jnp.exp(masked_prev - log_total[..., None])
    weights_own = probs_own.astype(jnp.bfloat16)
    weights_prev = probs_prev.astype(jnp.bfloat16)
    attended = (mix(weights_own, own_values) + mix(weights_prev, prev_values)).astype(jnp.bfloat16)
    row_delta = jnp.sum(grad_lanes.astype(jnp.float32) * attended.astype(jnp.float32), axis=-1)
    delta_cols = jnp.transpose(row_delta, (0, 2, 3, 1))
    sink_terms = -jnp.sum(jnp.exp(sink_col - log_total) * delta_cols, axis=(0, 3))
    sink_grad = all_sum(sink_terms.reshape(HEADS), ("ctx", "dp"))

    dscore_prev = (probs_prev * (grad_scores(prev_values) - delta_cols[..., None])).astype(
        jnp.bfloat16
    )
    prev_part = jnp.concatenate(
        [key_side(dscore_prev, query_lanes) * score_scale, key_side(weights_prev, grad_lanes)],
        axis=2,
    ).astype(jnp.bfloat16)
    dscore_own = (probs_own * (dprob_own - delta_cols[..., None])).astype(jnp.bfloat16)
    dquery = (mix(dscore_own, own_keys) + mix(dscore_prev, prev_keys)) * score_scale
    own_part = jnp.concatenate(
        [key_side(dscore_own, query_lanes) * score_scale, key_side(weights_own, grad_lanes)],
        axis=2,
    )

    send0, send1 = lax.optimization_barrier((prev_part[0], prev_part[1]))
    into0 = shift_down(send0, "ctx")
    into1 = shift_up(send1, "ctx")
    into0 = jnp.where(at_fold, prev_part[1], into0)
    gathered = own_part + jnp.stack([into0, into1]).astype(jnp.float32)

    out_shape = (1, 1, 2, block_rows, query_width)
    pair_out = (1, 1, 2, block_rows, value_width)
    attn_out = attended.reshape(out_shape)
    query_grad = dquery.astype(jnp.bfloat16).reshape(out_shape)
    key_grad = gathered[:, :, :value_width].astype(jnp.bfloat16).reshape(pair_out)
    value_grad = gathered[:, :, value_width:].astype(jnp.bfloat16).reshape(pair_out)
    return (attn_out, query_grad, key_grad, value_grad, sink_grad)


def solution(mesh):
    in_specs = (
        P("dp", "ctx", None, None, None),
        P("dp", "ctx", None, None, None),
        P("dp", "ctx", None, None, None),
        P("dp", "ctx", None, None, None),
        P(),
        P("dp", "ctx", None, None, None),
    )
    out_specs = (
        P("dp", "ctx", None, None, None),
        P("dp", "ctx", None, None, None),
        P("dp", "ctx", None, None, None),
        P("dp", "ctx", None, None, None),
        P(),
    )
    return jax.shard_map(
        per_device, mesh=mesh, in_specs=in_specs, out_specs=out_specs, check_vma=False
    )
```

```python
import math

import jax
import jax.numpy as jnp
from jax import lax
from jax.experimental import pallas as pl
from jax.experimental.pallas import tpu as pltpu
from jax.sharding import PartitionSpec as P

HEADS = 32
KV_HEADS = 4
HEAD_DIM = 128
GROUP = 8
REACH = 1


def shift_up(x, axis):
    size = lax.axis_size(axis)
    return lax.ppermute(x, axis, [(i, i + 1) for i in range(size - 1)])


def shift_down(x, axis):
    size = lax.axis_size(axis)
    return lax.ppermute(x, axis, [(i + 1, i) for i in range(size - 1)])


def all_sum(x, axes):
    count = 1
    for axis in axes:
        count *= lax.axis_size(axis)
    spread = jnp.broadcast_to(x[None], (count,) + x.shape)
    return jnp.sum(lax.all_to_all(spread, axes, 0, 0, tiled=True), axis=0)


def group_kernel(
    sink_ref, q_ref, g_ref, k_ref, v_ref, allow_ref, o_ref, dq_ref, dk_ref, dv_ref, st_ref
):
    group = pl.program_id(1)
    rows = q_ref.shape[1]
    score_scale = 1.0 / math.sqrt(HEAD_DIM)
    heads = [pl.ds(h * HEAD_DIM, HEAD_DIM) for h in range(GROUP)]
    query = jnp.concatenate([q_ref[0, :, cols] for cols in heads], axis=0)
    grad = jnp.concatenate([g_ref[0, :, cols] for cols in heads], axis=0)
    key = k_ref[0]
    value = v_ref[0]
    allowed = jnp.concatenate([allow_ref[0]] * GROUP, axis=0) > 0.5
    head_of_row = lax.broadcasted_iota(jnp.int32, (GROUP * rows, 1), 0) // rows
    sink = jnp.zeros((GROUP * rows, 1), jnp.float32)
    for h in range(GROUP):
        sink = jnp.where(head_of_row == h, sink_ref[group * GROUP + h], sink)
    contract_last = (((1,), (1,)), ((), ()))
    contract_first = (((0,), (0,)), ((), ()))
    scores = (
        lax.dot_general(query, key, contract_last, preferred_element_type=jnp.float32)
        * score_scale
    )
    masked = jnp.where(allowed, scores, -jnp.inf)
    row_top = jnp.maximum(sink, jnp.max(masked, axis=1, keepdims=True))
    row_total = jnp.exp(sink - row_top) + jnp.sum(
        jnp.exp(masked - row_top), axis=1, keepdims=True
    )
    log_total = row_top + jnp.log(row_total)
    probs = jnp.exp(masked - log_total)
    weights = probs.astype(jnp.bfloat16)
    attended = jnp.dot(weights, value, preferred_element_type=jnp.float32).astype(jnp.bfloat16)
    row_delta = jnp.sum(
        grad.astype(jnp.float32) * attended.astype(jnp.float32), axis=1, keepdims=True
    )
    dprob = lax.dot_general(grad, value, contract_last, preferred_element_type=jnp.float32)
    dscore = (probs * (dprob - row_delta)).astype(jnp.bfloat16)
    dquery = jnp.dot(dscore, key, preferred_element_type=jnp.float32) * score_scale
    dk_ref[0] = (
        lax.dot_general(dscore, query, contract_first, preferred_element_type=jnp.float32)
        * score_scale
    )
    dv_ref[0] = lax.dot_general(weights, grad, contract_first, preferred_element_type=jnp.float32)
    sink_share = jnp.exp(sink - log_total) * row_delta
    for h in range(GROUP):
        part = slice(h * rows, (h + 1) * rows)
        o_ref[0, :, heads[h]] = attended[part]
        dq_ref[0, :, heads[h]] = dquery[part].astype(jnp.bfloat16)
        total = -jnp.sum(sink_share[part], axis=0, keepdims=True)
        st_ref[0, 0, pl.ds(h, 1), :] = jnp.broadcast_to(total, (1, 128))


def attend_blocks(sink_logit, queries, out_grad, window, allowed):
    lanes, rows, query_width = queries.shape
    span = window.shape[1]
    group_width = GROUP * HEAD_DIM
    lane_rows = lambda lane, group: (lane, 0, group)
    flops = 2 * lanes * HEADS * rows * span * HEAD_DIM * 6
    moved = 2 * (4 * queries.size + 2 * window.size) + 4 * allowed.size + 8 * window.size
    return pl.pallas_call(
        group_kernel,
        grid=(lanes, KV_HEADS),
        in_specs=[
            pl.BlockSpec(memory_space=pltpu.SMEM),
            pl.BlockSpec((1, rows, group_width), lane_rows),
            pl.BlockSpec((1, rows, group_width), lane_rows),
            pl.BlockSpec((1, span, HEAD_DIM), lane_rows),
            pl.BlockSpec((1, span, HEAD_DIM), lambda lane, group: (lane, 0, KV_HEADS + group)),
            pl.BlockSpec((1, rows, span), lambda lane, group: (lane, 0, 0)),
        ],
        out_specs=[
            pl.BlockSpec((1, rows, group_width), lane_rows),
            pl.BlockSpec((1, rows, group_width), lane_rows),
            pl.BlockSpec((1, span, HEAD_DIM), lane_rows),
            pl.BlockSpec((1, span, HEAD_DIM), lane_rows),
            pl.BlockSpec((1, 1, GROUP, 128), lambda lane, group: (lane, group, 0, 0)),
        ],
        out_shape=[
            jax.ShapeDtypeStruct((lanes, rows, query_width), jnp.bfloat16),
            jax.ShapeDtypeStruct((lanes, rows, query_width), jnp.bfloat16),
            jax.ShapeDtypeStruct((lanes, span, KV_HEADS * HEAD_DIM), jnp.float32),
            jax.ShapeDtypeStruct((lanes, span, KV_HEADS * HEAD_DIM), jnp.float32),
            jax.ShapeDtypeStruct((lanes, KV_HEADS, GROUP, 128), jnp.float32),
        ],
        cost_estimate=pl.CostEstimate(
            flops=flops, transcendentals=2 * lanes * HEADS * rows * span, bytes_accessed=moved
        ),
    )(sink_logit, queries, out_grad, window, window, allowed)

def per_device(queries, keys, values, doc_bounds, sink_logit, out_grad):
    block_rows = queries.shape[3]
    query_width = queries.shape[4]
    value_width = keys.shape[4]
    pair_count = lax.axis_size("ctx")
    my_index = lax.axis_index("ctx")
    score_scale = 1.0 / math.sqrt(HEAD_DIM)
    at_fold = my_index == pair_count - 1
    last_block = 2 * pair_count - 1
    span = (REACH + 1) * block_rows

    own_pair = jnp.concatenate(
        [keys.reshape(2, block_rows, value_width), values.reshape(2, block_rows, value_width)], axis=2
    )
    send0, send1 = lax.optimization_barrier((own_pair[0], own_pair[1]))
    prev0 = shift_up(send0, "ctx")
    prev1 = shift_down(send1, "ctx")
    prev1 = jnp.where(at_fold, own_pair[0], prev1)
    prev_pair = jnp.stack([prev0, prev1])
    window = jnp.concatenate([prev_pair, own_pair], axis=1)

    lane_block = jnp.stack([my_index, last_block - my_index]).astype(jnp.int32)
    row_offsets = jnp.arange(block_rows, dtype=jnp.int32)
    window_offsets = jnp.arange(span, dtype=jnp.int32)
    query_pos = lane_block[:, None] * block_rows + row_offsets[None, :]
    key_pos = (lane_block[:, None] - REACH) * block_rows + window_offsets[None, :]
    first_pos = doc_bounds.reshape(2, 2, block_rows)[:, 0]
    allowed = (key_pos[:, None, :] <= query_pos[:, :, None]) & (
        key_pos[:, None, :] >= first_pos[:, :, None]
    )
    attended, dquery, key_part, value_part, sink_parts = attend_blocks(
        sink_logit,
        queries.reshape(2, block_rows, query_width),
        out_grad.reshape(2, block_rows, query_width),
        window,
        allowed.astype(jnp.float32),
    )
    sink_terms = jnp.sum(sink_parts[:, :, :, 0], axis=0)
    sink_grad = all_sum(sink_terms.reshape(HEADS), ("ctx", "dp"))
    partial = jnp.concatenate([key_part, value_part], axis=2)

    prev_part = partial[:, :block_rows].astype(jnp.bfloat16)
    send0, send1 = lax.optimization_barrier((prev_part[0], prev_part[1]))
    into0 = shift_down(send0, "ctx")
    into1 = shift_up(send1, "ctx")
    into0 = jnp.where(at_fold, prev_part[1], into0)
    own_part = partial[:, block_rows:]
    gathered = own_part + jnp.stack([into0, into1]).astype(jnp.float32)

    out_shape = (1, 1, 2, block_rows, query_width)
    pair_out = (1, 1, 2, block_rows, value_width)
    attn_out = attended.reshape(out_shape)
    query_grad = dquery.reshape(out_shape)
    key_grad = gathered[:, :, :value_width].astype(jnp.bfloat16).reshape(pair_out)
    value_grad = gathered[:, :, value_width:].astype(jnp.bfloat16).reshape(pair_out)
    return (attn_out, query_grad, key_grad, value_grad, sink_grad)


def solution(mesh):
    in_specs = (
        P("dp", "ctx", None, None, None),
        P("dp", "ctx", None, None, None),
        P("dp", "ctx", None, None, None),
        P("dp", "ctx", None, None, None),
        P(),
        P("dp", "ctx", None, None, None),
    )
    out_specs = (
        P("dp", "ctx", None, None, None),
        P("dp", "ctx", None, None, None),
        P("dp", "ctx", None, None, None),
        P("dp", "ctx", None, None, None),
        P(),
    )
    return jax.shard_map(
        per_device, mesh=mesh, in_specs=in_specs, out_specs=out_specs, check_vma=False
    )
```

```python
import math

import jax
import jax.numpy as jnp
from jax import lax
from jax.experimental import pallas as pl
from jax.experimental.pallas import tpu as pltpu
from jax.sharding import PartitionSpec as P

HEADS = 32
KV_HEADS = 4
HEAD_DIM = 128
GROUP = 8
REACH = 1


def shift_up(x, axis):
    size = lax.axis_size(axis)
    return lax.ppermute(x, axis, [(i, i + 1) for i in range(size - 1)])


def shift_down(x, axis):
    size = lax.axis_size(axis)
    return lax.ppermute(x, axis, [(i + 1, i) for i in range(size - 1)])


def all_sum(x, axes):
    count = 1
    for axis in axes:
        count *= lax.axis_size(axis)
    spread = jnp.broadcast_to(x[None], (count,) + x.shape)
    return jnp.sum(lax.all_to_all(spread, axes, 0, 0, tiled=True), axis=0)


def group_kernel(
    sink_ref, q_ref, g_ref, k_ref, v_ref, allow_ref, o_ref, dq_ref, msg_ref, own_ref, st_ref
):
    group = pl.program_id(1)
    rows = q_ref.shape[1]
    score_scale = 1.0 / math.sqrt(HEAD_DIM)
    heads = [pl.ds(h * HEAD_DIM, HEAD_DIM) for h in range(GROUP)]
    query = jnp.concatenate([q_ref[0, :, cols] for cols in heads], axis=0)
    grad = jnp.concatenate([g_ref[0, :, cols] for cols in heads], axis=0)
    key = k_ref[0]
    value = v_ref[0]
    allowed = jnp.concatenate([allow_ref[0]] * GROUP, axis=0) > 0.5
    head_of_row = lax.broadcasted_iota(jnp.int32, (GROUP * rows, 1), 0) // rows
    sink = jnp.zeros((GROUP * rows, 1), jnp.float32)
    for h in range(GROUP):
        sink = jnp.where(head_of_row == h, sink_ref[group * GROUP + h], sink)
    contract_last = (((1,), (1,)), ((), ()))
    contract_first = (((0,), (0,)), ((), ()))
    scores = (
        lax.dot_general(query, key, contract_last, preferred_element_type=jnp.float32)
        * score_scale
    )
    masked = jnp.where(allowed, scores, -jnp.inf)
    row_top = jnp.maximum(sink, jnp.max(masked, axis=1, keepdims=True))
    row_total = jnp.exp(sink - row_top) + jnp.sum(
        jnp.exp(masked - row_top), axis=1, keepdims=True
    )
    log_total = row_top + jnp.log(row_total)
    probs = jnp.exp(masked - log_total)
    weights = probs.astype(jnp.bfloat16)
    attended = jnp.dot(weights, value, preferred_element_type=jnp.float32).astype(jnp.bfloat16)
    row_delta = jnp.sum(
        grad.astype(jnp.float32) * attended.astype(jnp.float32), axis=1, keepdims=True
    )
    dprob = lax.dot_general(grad, value, contract_last, preferred_element_type=jnp.float32)
    dscore = (probs * (dprob - row_delta)).astype(jnp.bfloat16)
    dquery = jnp.dot(dscore, key, preferred_element_type=jnp.float32) * score_scale
    dkey = (
        lax.dot_general(dscore, query, contract_first, preferred_element_type=jnp.float32)
        * score_scale
    )
    dvalue = lax.dot_general(weights, grad, contract_first, preferred_element_type=jnp.float32)
    msg_ref[0, :, pl.ds(0, HEAD_DIM)] = dkey[:rows].astype(jnp.bfloat16)
    msg_ref[0, :, pl.ds(HEAD_DIM, HEAD_DIM)] = dvalue[:rows].astype(jnp.bfloat16)
    own_ref[0, :, pl.ds(0, HEAD_DIM)] = dkey[rows:]
    own_ref[0, :, pl.ds(HEAD_DIM, HEAD_DIM)] = dvalue[rows:]
    sink_share = jnp.exp(sink - log_total) * row_delta
    lane = lax.broadcasted_iota(jnp.int32, (1, 128), 1)
    sink_row = jnp.zeros((1, 128), jnp.float32)
    for h in range(GROUP):
        part = slice(h * rows, (h + 1) * rows)
        o_ref[0, :, heads[h]] = attended[part]
        dq_ref[0, :, heads[h]] = dquery[part].astype(jnp.bfloat16)
        total = -jnp.sum(sink_share[part], axis=0, keepdims=True)
        sink_row = jnp.where(lane == group * GROUP + h, total, sink_row)

    @pl.when((pl.program_id(0) == 0) & (group == 0))
    def _():
        st_ref[...] = jnp.zeros_like(st_ref)

    st_ref[pl.ds(0, 1), :] += sink_row


def attend_blocks(sink_logit, queries, out_grad, window, allowed):
    lanes, rows, query_width = queries.shape
    span = window.shape[1]
    group_width = GROUP * HEAD_DIM
    lane_rows = lambda lane, group: (lane, 0, group)
    flops = 2 * lanes * HEADS * rows * span * HEAD_DIM * 6
    moved = 2 * (4 * queries.size + 2 * window.size) + 4 * allowed.size + 8 * window.size
    return pl.pallas_call(
        group_kernel,
        grid=(lanes, KV_HEADS),
        in_specs=[
            pl.BlockSpec(memory_space=pltpu.SMEM),
            pl.BlockSpec((1, rows, group_width), lane_rows),
            pl.BlockSpec((1, rows, group_width), lane_rows),
            pl.BlockSpec((1, span, HEAD_DIM), lane_rows),
            pl.BlockSpec((1, span, HEAD_DIM), lambda lane, group: (lane, 0, KV_HEADS + group)),
            pl.BlockSpec((1, rows, span), lambda lane, group: (lane, 0, 0)),
        ],
        out_specs=[
            pl.BlockSpec((1, rows, group_width), lane_rows),
            pl.BlockSpec((1, rows, group_width), lane_rows),
            pl.BlockSpec((1, rows, 2 * HEAD_DIM), lane_rows),
            pl.BlockSpec((1, rows, 2 * HEAD_DIM), lane_rows),
            pl.BlockSpec((8, 128), lambda lane, group: (0, 0)),
        ],
        out_shape=[
            jax.ShapeDtypeStruct((lanes, rows, query_width), jnp.bfloat16),
            jax.ShapeDtypeStruct((lanes, rows, query_width), jnp.bfloat16),
            jax.ShapeDtypeStruct((lanes, rows, 2 * KV_HEADS * HEAD_DIM), jnp.bfloat16),
            jax.ShapeDtypeStruct((lanes, rows, 2 * KV_HEADS * HEAD_DIM), jnp.float32),
            jax.ShapeDtypeStruct((8, 128), jnp.float32),
        ],
        cost_estimate=pl.CostEstimate(
            flops=flops, transcendentals=2 * lanes * HEADS * rows * span, bytes_accessed=moved
        ),
    )(sink_logit, queries, out_grad, window, window, allowed)

def per_device(queries, keys, values, doc_bounds, sink_logit, out_grad):
    block_rows = queries.shape[3]
    query_width = queries.shape[4]
    value_width = keys.shape[4]
    pair_count = lax.axis_size("ctx")
    my_index = lax.axis_index("ctx")
    score_scale = 1.0 / math.sqrt(HEAD_DIM)
    at_fold = my_index == pair_count - 1
    last_block = 2 * pair_count - 1
    span = (REACH + 1) * block_rows

    own_pair = jnp.concatenate(
        [keys.reshape(2, block_rows, value_width), values.reshape(2, block_rows, value_width)], axis=2
    )
    send0, send1 = lax.optimization_barrier((own_pair[0], own_pair[1]))
    prev0 = shift_up(send0, "ctx")
    prev1 = shift_down(send1, "ctx")
    prev1 = jnp.where(at_fold, own_pair[0], prev1)
    prev_pair = jnp.stack([prev0, prev1])
    window = jnp.concatenate([prev_pair, own_pair], axis=1)

    lane_block = jnp.stack([my_index, last_block - my_index]).astype(jnp.int32)
    row_offsets = jnp.arange(block_rows, dtype=jnp.int32)
    window_offsets = jnp.arange(span, dtype=jnp.int32)
    query_pos = lane_block[:, None] * block_rows + row_offsets[None, :]
    key_pos = (lane_block[:, None] - REACH) * block_rows + window_offsets[None, :]
    first_pos = doc_bounds.reshape(2, 2, block_rows)[:, 0]
    allowed = (key_pos[:, None, :] <= query_pos[:, :, None]) & (
        key_pos[:, None, :] >= first_pos[:, :, None]
    )
    attended, dquery, message, own_part, sink_row = attend_blocks(
        sink_logit,
        queries.reshape(2, block_rows, query_width),
        out_grad.reshape(2, block_rows, query_width),
        window,
        allowed.astype(jnp.float32),
    )
    sink_grad = all_sum(sink_row[0, :HEADS], ("ctx", "dp"))

    send0, send1 = lax.optimization_barrier((message[0], message[1]))
    into0 = shift_down(send0, "ctx")
    into1 = shift_up(send1, "ctx")
    into0 = jnp.where(at_fold, message[1], into0)
    gathered = own_part + jnp.stack([into0, into1]).astype(jnp.float32)
    gathered = gathered.reshape(2, block_rows, KV_HEADS, 2, HEAD_DIM)

    out_shape = (1, 1, 2, block_rows, query_width)
    pair_out = (1, 1, 2, block_rows, value_width)
    attn_out = attended.reshape(out_shape)
    query_grad = dquery.reshape(out_shape)
    key_grad = gathered[:, :, :, 0].astype(jnp.bfloat16).reshape(pair_out)
    value_grad = gathered[:, :, :, 1].astype(jnp.bfloat16).reshape(pair_out)
    return (attn_out, query_grad, key_grad, value_grad, sink_grad)


def solution(mesh):
    in_specs = (
        P("dp", "ctx", None, None, None),
        P("dp", "ctx", None, None, None),
        P("dp", "ctx", None, None, None),
        P("dp", "ctx", None, None, None),
        P(),
        P("dp", "ctx", None, None, None),
    )
    out_specs = (
        P("dp", "ctx", None, None, None),
        P("dp", "ctx", None, None, None),
        P("dp", "ctx", None, None, None),
        P("dp", "ctx", None, None, None),
        P(),
    )
    return jax.shard_map(
        per_device, mesh=mesh, in_specs=in_specs, out_specs=out_specs, check_vma=False
    )
```

```python
import math

import jax
import jax.numpy as jnp
from jax import lax
from jax.experimental import pallas as pl
from jax.experimental.pallas import tpu as pltpu
from jax.sharding import PartitionSpec as P

HEADS = 32
KV_HEADS = 4
HEAD_DIM = 128
GROUP = 8
REACH = 1


def shift_up(x, axis):
    size = lax.axis_size(axis)
    return lax.ppermute(x, axis, [(i, i + 1) for i in range(size - 1)])


def shift_down(x, axis):
    size = lax.axis_size(axis)
    return lax.ppermute(x, axis, [(i + 1, i) for i in range(size - 1)])


def swap_pairs(x, axis, offset):
    size = lax.axis_size(axis)
    pairs = []
    for i in range(size):
        partner = i + 1 if (i - offset) % 2 == 0 else i - 1
        if 0 <= partner < size:
            pairs.append((i, partner))
    return lax.ppermute(x, axis, pairs)


def neighbour_swap(to_next, to_prev, axis):
    even = lax.axis_index(axis) % 2 == 0
    first, second = lax.optimization_barrier(
        (jnp.where(even, to_next, to_prev), jnp.where(even, to_prev, to_next))
    )
    got_first = swap_pairs(first, axis, 0)
    got_second = swap_pairs(second, axis, 1)
    from_prev = jnp.where(even, got_second, got_first)
    from_next = jnp.where(even, got_first, got_second)
    return from_prev, from_next


def all_sum(x, axes):
    count = 1
    for axis in axes:
        count *= lax.axis_size(axis)
    spread = jnp.broadcast_to(x[None], (count,) + x.shape)
    return jnp.sum(lax.all_to_all(spread, axes, 0, 0, tiled=True), axis=0)


def group_kernel(
    sink_ref, q_ref, g_ref, k_ref, v_ref, allow_ref, o_ref, dq_ref, dk_ref, dv_ref, st_ref
):
    group = pl.program_id(1)
    rows = q_ref.shape[1]
    score_scale = 1.0 / math.sqrt(HEAD_DIM)
    heads = [pl.ds(h * HEAD_DIM, HEAD_DIM) for h in range(GROUP)]
    query = jnp.concatenate([q_ref[0, :, cols] for cols in heads], axis=0)
    grad = jnp.concatenate([g_ref[0, :, cols] for cols in heads], axis=0)
    key = k_ref[0]
    value = v_ref[0]
    allowed = jnp.concatenate([allow_ref[0]] * GROUP, axis=0) > 0.5
    head_of_row = lax.broadcasted_iota(jnp.int32, (GROUP * rows, 1), 0) // rows
    sink = jnp.zeros((GROUP * rows, 1), jnp.float32)
    for h in range(GROUP):
        sink = jnp.where(head_of_row == h, sink_ref[group * GROUP + h], sink)
    contract_last = (((1,), (1,)), ((), ()))
    contract_first = (((0,), (0,)), ((), ()))
    scores = (
        lax.dot_general(query, key, contract_last, preferred_element_type=jnp.float32)
        * score_scale
    )
    masked = jnp.where(allowed, scores, -jnp.inf)
    row_top = jnp.maximum(sink, jnp.max(masked, axis=1, keepdims=True))
    row_total = jnp.exp(sink - row_top) + jnp.sum(
        jnp.exp(masked - row_top), axis=1, keepdims=True
    )
    log_total = row_top + jnp.log(row_total)
    probs = jnp.exp(masked - log_total)
    weights = probs.astype(jnp.bfloat16)
    attended = jnp.dot(weights, value, preferred_element_type=jnp.float32).astype(jnp.bfloat16)
    row_delta = jnp.sum(
        grad.astype(jnp.float32) * attended.astype(jnp.float32), axis=1, keepdims=True
    )
    dprob = lax.dot_general(grad, value, contract_last, preferred_element_type=jnp.float32)
    dscore = (probs * (dprob - row_delta)).astype(jnp.bfloat16)
    dquery = jnp.dot(dscore, key, preferred_element_type=jnp.float32) * score_scale
    dk_ref[0] = (
        lax.dot_general(dscore, query, contract_first, preferred_element_type=jnp.float32)
        * score_scale
    )
    dv_ref[0] = lax.dot_general(weights, grad, contract_first, preferred_element_type=jnp.float32)
    sink_share = jnp.exp(sink - log_total) * row_delta
    for h in range(GROUP):
        part = slice(h * rows, (h + 1) * rows)
        o_ref[0, :, heads[h]] = attended[part]
        dq_ref[0, :, heads[h]] = dquery[part].astype(jnp.bfloat16)
        total = -jnp.sum(sink_share[part], axis=0, keepdims=True)
        st_ref[0, 0, pl.ds(h, 1), :] = jnp.broadcast_to(total, (1, 128))


def attend_blocks(sink_logit, queries, out_grad, window, allowed):
    lanes, rows, query_width = queries.shape
    span = window.shape[1]
    group_width = GROUP * HEAD_DIM
    lane_rows = lambda lane, group: (lane, 0, group)
    flops = 2 * lanes * HEADS * rows * span * HEAD_DIM * 6
    moved = 2 * (4 * queries.size + 2 * window.size) + 4 * allowed.size + 8 * window.size
    return pl.pallas_call(
        group_kernel,
        grid=(lanes, KV_HEADS),
        in_specs=[
            pl.BlockSpec(memory_space=pltpu.SMEM),
            pl.BlockSpec((1, rows, group_width), lane_rows),
            pl.BlockSpec((1, rows, group_width), lane_rows),
            pl.BlockSpec((1, span, HEAD_DIM), lane_rows),
            pl.BlockSpec((1, span, HEAD_DIM), lambda lane, group: (lane, 0, KV_HEADS + group)),
            pl.BlockSpec((1, rows, span), lambda lane, group: (lane, 0, 0)),
        ],
        out_specs=[
            pl.BlockSpec((1, rows, group_width), lane_rows),
            pl.BlockSpec((1, rows, group_width), lane_rows),
            pl.BlockSpec((1, span, HEAD_DIM), lane_rows),
            pl.BlockSpec((1, span, HEAD_DIM), lane_rows),
            pl.BlockSpec((1, 1, GROUP, 128), lambda lane, group: (lane, group, 0, 0)),
        ],
        out_shape=[
            jax.ShapeDtypeStruct((lanes, rows, query_width), jnp.bfloat16),
            jax.ShapeDtypeStruct((lanes, rows, query_width), jnp.bfloat16),
            jax.ShapeDtypeStruct((lanes, span, KV_HEADS * HEAD_DIM), jnp.float32),
            jax.ShapeDtypeStruct((lanes, span, KV_HEADS * HEAD_DIM), jnp.float32),
            jax.ShapeDtypeStruct((lanes, KV_HEADS, GROUP, 128), jnp.float32),
        ],
        cost_estimate=pl.CostEstimate(
            flops=flops, transcendentals=2 * lanes * HEADS * rows * span, bytes_accessed=moved
        ),
    )(sink_logit, queries, out_grad, window, window, allowed)

def per_device(queries, keys, values, doc_bounds, sink_logit, out_grad):
    block_rows = queries.shape[3]
    query_width = queries.shape[4]
    value_width = keys.shape[4]
    pair_count = lax.axis_size("ctx")
    my_index = lax.axis_index("ctx")
    score_scale = 1.0 / math.sqrt(HEAD_DIM)
    at_fold = my_index == pair_count - 1
    last_block = 2 * pair_count - 1
    span = (REACH + 1) * block_rows

    own_pair = jnp.concatenate(
        [keys.reshape(2, block_rows, value_width), values.reshape(2, block_rows, value_width)], axis=2
    )
    prev0, prev1 = neighbour_swap(own_pair[0], own_pair[1], "ctx")
    prev1 = jnp.where(at_fold, own_pair[0], prev1)
    prev_pair = jnp.stack([prev0, prev1])
    window = jnp.concatenate([prev_pair, own_pair], axis=1)

    lane_block = jnp.stack([my_index, last_block - my_index]).astype(jnp.int32)
    row_offsets = jnp.arange(block_rows, dtype=jnp.int32)
    window_offsets = jnp.arange(span, dtype=jnp.int32)
    query_pos = lane_block[:, None] * block_rows + row_offsets[None, :]
    key_pos = (lane_block[:, None] - REACH) * block_rows + window_offsets[None, :]
    first_pos = doc_bounds.reshape(2, 2, block_rows)[:, 0]
    allowed = (key_pos[:, None, :] <= query_pos[:, :, None]) & (
        key_pos[:, None, :] >= first_pos[:, :, None]
    )
    attended, dquery, key_part, value_part, sink_parts = attend_blocks(
        sink_logit,
        queries.reshape(2, block_rows, query_width),
        out_grad.reshape(2, block_rows, query_width),
        window,
        allowed.astype(jnp.float32),
    )
    sink_terms = jnp.sum(sink_parts[:, :, :, 0], axis=0)
    sink_grad = all_sum(sink_terms.reshape(HEADS), ("ctx", "dp"))
    partial = jnp.concatenate([key_part, value_part], axis=2)

    prev_part = partial[:, :block_rows].astype(jnp.bfloat16)
    into1, into0 = neighbour_swap(prev_part[1], prev_part[0], "ctx")
    into0 = jnp.where(at_fold, prev_part[1], into0)
    own_part = partial[:, block_rows:]
    gathered = own_part + jnp.stack([into0, into1]).astype(jnp.float32)

    out_shape = (1, 1, 2, block_rows, query_width)
    pair_out = (1, 1, 2, block_rows, value_width)
    attn_out = attended.reshape(out_shape)
    query_grad = dquery.reshape(out_shape)
    key_grad = gathered[:, :, :value_width].astype(jnp.bfloat16).reshape(pair_out)
    value_grad = gathered[:, :, value_width:].astype(jnp.bfloat16).reshape(pair_out)
    return (attn_out, query_grad, key_grad, value_grad, sink_grad)


def solution(mesh):
    in_specs = (
        P("dp", "ctx", None, None, None),
        P("dp", "ctx", None, None, None),
        P("dp", "ctx", None, None, None),
        P("dp", "ctx", None, None, None),
        P(),
        P("dp", "ctx", None, None, None),
    )
    out_specs = (
        P("dp", "ctx", None, None, None),
        P("dp", "ctx", None, None, None),
        P("dp", "ctx", None, None, None),
        P("dp", "ctx", None, None, None),
        P(),
    )
    return jax.shard_map(
        per_device, mesh=mesh, in_specs=in_specs, out_specs=out_specs, check_vma=False
    )
```

```python
import math

import jax
import jax.numpy as jnp
from jax import lax
from jax.experimental import pallas as pl
from jax.experimental.pallas import tpu as pltpu
from jax.sharding import PartitionSpec as P

HEADS = 32
KV_HEADS = 4
HEAD_DIM = 128
GROUP = 8
REACH = 1


def shift_up(x, axis):
    size = lax.axis_size(axis)
    return lax.ppermute(x, axis, [(i, i + 1) for i in range(size - 1)])


def shift_down(x, axis):
    size = lax.axis_size(axis)
    return lax.ppermute(x, axis, [(i + 1, i) for i in range(size - 1)])


def swap_pairs(x, axis, offset):
    size = lax.axis_size(axis)
    pairs = []
    for i in range(size):
        partner = i + 1 if (i - offset) % 2 == 0 else i - 1
        if 0 <= partner < size:
            pairs.append((i, partner))
    return lax.ppermute(x, axis, pairs)


def neighbour_swap(to_next, to_prev, axis):
    even = lax.axis_index(axis) % 2 == 0
    first, second = lax.optimization_barrier(
        (jnp.where(even, to_next, to_prev), jnp.where(even, to_prev, to_next))
    )
    got_first = swap_pairs(first, axis, 0)
    got_second = swap_pairs(second, axis, 1)
    from_prev = jnp.where(even, got_second, got_first)
    from_next = jnp.where(even, got_first, got_second)
    return from_prev, from_next


def all_sum(x, axes):
    count = 1
    for axis in axes:
        count *= lax.axis_size(axis)
    spread = jnp.broadcast_to(x[None], (count,) + x.shape)
    return jnp.sum(lax.all_to_all(spread, axes, 0, 0, tiled=True), axis=0)


def group_kernel(
    sink_ref, q_ref, g_ref, k_ref, v_ref, allow_ref, o_ref, dq_ref, dk_ref, dv_ref, st_ref
):
    rows = q_ref.shape[1]
    score_scale = 1.0 / math.sqrt(HEAD_DIM)
    contract_last = (((1,), (1,)), ((), ()))
    contract_first = (((0,), (0,)), ((), ()))
    allowed = jnp.concatenate([allow_ref[0]] * GROUP, axis=0) > 0.5
    head_of_row = lax.broadcasted_iota(jnp.int32, (GROUP * rows, 1), 0) // rows
    for group in range(KV_HEADS):
        heads = [pl.ds((group * GROUP + h) * HEAD_DIM, HEAD_DIM) for h in range(GROUP)]
        side = pl.ds(group * HEAD_DIM, HEAD_DIM)
        query = jnp.concatenate([q_ref[0, :, cols] for cols in heads], axis=0)
        grad = jnp.concatenate([g_ref[0, :, cols] for cols in heads], axis=0)
        key = k_ref[0, :, side]
        value = v_ref[0, :, side]
        sink = jnp.zeros((GROUP * rows, 1), jnp.float32)
        for h in range(GROUP):
            sink = jnp.where(head_of_row == h, sink_ref[group * GROUP + h], sink)
        scores = (
            lax.dot_general(query, key, contract_last, preferred_element_type=jnp.float32)
            * score_scale
        )
        masked = jnp.where(allowed, scores, -jnp.inf)
        row_top = jnp.maximum(sink, jnp.max(masked, axis=1, keepdims=True))
        row_total = jnp.exp(sink - row_top) + jnp.sum(
            jnp.exp(masked - row_top), axis=1, keepdims=True
        )
        log_total = row_top + jnp.log(row_total)
        probs = jnp.exp(masked - log_total)
        weights = probs.astype(jnp.bfloat16)
        attended = jnp.dot(weights, value, preferred_element_type=jnp.float32).astype(
            jnp.bfloat16
        )
        row_delta = jnp.sum(
            grad.astype(jnp.float32) * attended.astype(jnp.float32), axis=1, keepdims=True
        )
        dprob = lax.dot_general(grad, value, contract_last, preferred_element_type=jnp.float32)
        dscore = (probs * (dprob - row_delta)).astype(jnp.bfloat16)
        dquery = jnp.dot(dscore, key, preferred_element_type=jnp.float32) * score_scale
        dk_ref[0, :, side] = (
            lax.dot_general(dscore, query, contract_first, preferred_element_type=jnp.float32)
            * score_scale
        )
        dv_ref[0, :, side] = lax.dot_general(
            weights, grad, contract_first, preferred_element_type=jnp.float32
        )
        sink_share = jnp.exp(sink - log_total) * row_delta
        for h in range(GROUP):
            part = slice(h * rows, (h + 1) * rows)
            o_ref[0, :, heads[h]] = attended[part]
            dq_ref[0, :, heads[h]] = dquery[part].astype(jnp.bfloat16)
            total = -jnp.sum(sink_share[part], axis=0, keepdims=True)
            st_ref[0, group, pl.ds(h, 1), :] = jnp.broadcast_to(total, (1, 128))


def attend_blocks(sink_logit, queries, out_grad, window, allowed):
    lanes, rows, query_width = queries.shape
    span = window.shape[1]
    side_width = KV_HEADS * HEAD_DIM
    row_spec = pl.BlockSpec((1, rows, query_width), lambda lane: (lane, 0, 0))
    side_spec = pl.BlockSpec((1, span, side_width), lambda lane: (lane, 0, 0))
    flops = 2 * lanes * HEADS * rows * span * HEAD_DIM * 6
    moved = 2 * (4 * queries.size + 2 * window.size) + 4 * allowed.size + 8 * window.size
    return pl.pallas_call(
        group_kernel,
        grid=(lanes,),
        in_specs=[
            pl.BlockSpec(memory_space=pltpu.SMEM),
            row_spec,
            row_spec,
            side_spec,
            pl.BlockSpec((1, span, side_width), lambda lane: (lane, 0, 1)),
            pl.BlockSpec((1, rows, span), lambda lane: (lane, 0, 0)),
        ],
        out_specs=[
            row_spec,
            row_spec,
            side_spec,
            side_spec,
            pl.BlockSpec((1, KV_HEADS, GROUP, 128), lambda lane: (lane, 0, 0, 0)),
        ],
        out_shape=[
            jax.ShapeDtypeStruct((lanes, rows, query_width), jnp.bfloat16),
            jax.ShapeDtypeStruct((lanes, rows, query_width), jnp.bfloat16),
            jax.ShapeDtypeStruct((lanes, span, side_width), jnp.float32),
            jax.ShapeDtypeStruct((lanes, span, side_width), jnp.float32),
            jax.ShapeDtypeStruct((lanes, KV_HEADS, GROUP, 128), jnp.float32),
        ],
        cost_estimate=pl.CostEstimate(
            flops=flops, transcendentals=2 * lanes * HEADS * rows * span, bytes_accessed=moved
        ),
    )(sink_logit, queries, out_grad, window, window, allowed)


def per_device(queries, keys, values, doc_bounds, sink_logit, out_grad):
    block_rows = queries.shape[3]
    query_width = queries.shape[4]
    value_width = keys.shape[4]
    pair_count = lax.axis_size("ctx")
    my_index = lax.axis_index("ctx")
    score_scale = 1.0 / math.sqrt(HEAD_DIM)
    at_fold = my_index == pair_count - 1
    last_block = 2 * pair_count - 1
    span = (REACH + 1) * block_rows

    own_pair = jnp.concatenate(
        [keys.reshape(2, block_rows, value_width), values.reshape(2, block_rows, value_width)], axis=2
    )
    prev0, prev1 = neighbour_swap(own_pair[0], own_pair[1], "ctx")
    prev1 = jnp.where(at_fold, own_pair[0], prev1)
    prev_pair = jnp.stack([prev0, prev1])
    window = jnp.concatenate([prev_pair, own_pair], axis=1)

    lane_block = jnp.stack([my_index, last_block - my_index]).astype(jnp.int32)
    row_offsets = jnp.arange(block_rows, dtype=jnp.int32)
    window_offsets = jnp.arange(span, dtype=jnp.int32)
    query_pos = lane_block[:, None] * block_rows + row_offsets[None, :]
    key_pos = (lane_block[:, None] - REACH) * block_rows + window_offsets[None, :]
    first_pos = doc_bounds.reshape(2, 2, block_rows)[:, 0]
    allowed = (key_pos[:, None, :] <= query_pos[:, :, None]) & (
        key_pos[:, None, :] >= first_pos[:, :, None]
    )
    attended, dquery, key_part, value_part, sink_parts = attend_blocks(
        sink_logit,
        queries.reshape(2, block_rows, query_width),
        out_grad.reshape(2, block_rows, query_width),
        window,
        allowed.astype(jnp.float32),
    )
    sink_terms = jnp.sum(sink_parts[:, :, :, 0], axis=0)
    sink_grad = all_sum(sink_terms.reshape(HEADS), ("ctx", "dp"))
    partial = jnp.concatenate([key_part, value_part], axis=2)

    prev_part = partial[:, :block_rows].astype(jnp.bfloat16)
    into1, into0 = neighbour_swap(prev_part[1], prev_part[0], "ctx")
    into0 = jnp.where(at_fold, prev_part[1], into0)
    own_part = partial[:, block_rows:]
    gathered = own_part + jnp.stack([into0, into1]).astype(jnp.float32)

    out_shape = (1, 1, 2, block_rows, query_width)
    pair_out = (1, 1, 2, block_rows, value_width)
    attn_out = attended.reshape(out_shape)
    query_grad = dquery.reshape(out_shape)
    key_grad = gathered[:, :, :value_width].astype(jnp.bfloat16).reshape(pair_out)
    value_grad = gathered[:, :, value_width:].astype(jnp.bfloat16).reshape(pair_out)
    return (attn_out, query_grad, key_grad, value_grad, sink_grad)


def solution(mesh):
    in_specs = (
        P("dp", "ctx", None, None, None),
        P("dp", "ctx", None, None, None),
        P("dp", "ctx", None, None, None),
        P("dp", "ctx", None, None, None),
        P(),
        P("dp", "ctx", None, None, None),
    )
    out_specs = (
        P("dp", "ctx", None, None, None),
        P("dp", "ctx", None, None, None),
        P("dp", "ctx", None, None, None),
        P("dp", "ctx", None, None, None),
        P(),
    )
    return jax.shard_map(
        per_device, mesh=mesh, in_specs=in_specs, out_specs=out_specs, check_vma=False
    )
```

```python
import math

import jax
import jax.numpy as jnp
from jax import lax
from jax.experimental import pallas as pl
from jax.experimental.pallas import tpu as pltpu
from jax.sharding import PartitionSpec as P

HEADS = 32
KV_HEADS = 4
HEAD_DIM = 128
GROUP = 8
REACH = 1


def shift_up(x, axis):
    size = lax.axis_size(axis)
    return lax.ppermute(x, axis, [(i, i + 1) for i in range(size - 1)])


def shift_down(x, axis):
    size = lax.axis_size(axis)
    return lax.ppermute(x, axis, [(i + 1, i) for i in range(size - 1)])


def swap_pairs(x, axis, offset):
    size = lax.axis_size(axis)
    pairs = []
    for i in range(size):
        partner = i + 1 if (i - offset) % 2 == 0 else i - 1
        if 0 <= partner < size:
            pairs.append((i, partner))
    return lax.ppermute(x, axis, pairs)


def neighbour_swap(to_next, to_prev, axis):
    even = lax.axis_index(axis) % 2 == 0
    first, second = lax.optimization_barrier(
        (jnp.where(even, to_next, to_prev), jnp.where(even, to_prev, to_next))
    )
    got_first = swap_pairs(first, axis, 0)
    got_second = swap_pairs(second, axis, 1)
    from_prev = jnp.where(even, got_second, got_first)
    from_next = jnp.where(even, got_first, got_second)
    return from_prev, from_next


def all_sum(x, axes):
    count = 1
    for axis in axes:
        count *= lax.axis_size(axis)
    spread = jnp.broadcast_to(x[None], (count,) + x.shape)
    return jnp.sum(lax.all_to_all(spread, axes, 0, 0, tiled=True), axis=0)


def group_kernel(
    sink_ref, q_ref, g_ref, own_ref, prev_ref, allow_ref,
    o_ref, dq_ref, msg_ref, dk_ref, dv_ref, st_ref,
):
    rows = q_ref.shape[1]
    score_scale = 1.0 / math.sqrt(HEAD_DIM)
    contract_last = (((1,), (1,)), ((), ()))
    contract_first = (((0,), (0,)), ((), ()))
    allowed = jnp.concatenate([allow_ref[0]] * GROUP, axis=0) > 0.5
    head_of_row = lax.broadcasted_iota(jnp.int32, (GROUP * rows, 1), 0) // rows
    for group in range(KV_HEADS):
        heads = [pl.ds((group * GROUP + h) * HEAD_DIM, HEAD_DIM) for h in range(GROUP)]
        side = pl.ds(group * HEAD_DIM, HEAD_DIM)
        value_side = pl.ds((KV_HEADS + group) * HEAD_DIM, HEAD_DIM)
        query = jnp.concatenate([q_ref[0, :, cols] for cols in heads], axis=0)
        grad = jnp.concatenate([g_ref[0, :, cols] for cols in heads], axis=0)
        key = jnp.concatenate([prev_ref[0, :, side], own_ref[0, :, side]], axis=0)
        value = jnp.concatenate([prev_ref[0, :, value_side], own_ref[0, :, value_side]], axis=0)
        sink = jnp.zeros((GROUP * rows, 1), jnp.float32)
        for h in range(GROUP):
            sink = jnp.where(head_of_row == h, sink_ref[group * GROUP + h], sink)
        scores = (
            lax.dot_general(query, key, contract_last, preferred_element_type=jnp.float32)
            * score_scale
        )
        masked = jnp.where(allowed, scores, -jnp.inf)
        row_top = jnp.maximum(sink, jnp.max(masked, axis=1, keepdims=True))
        row_total = jnp.exp(sink - row_top) + jnp.sum(
            jnp.exp(masked - row_top), axis=1, keepdims=True
        )
        log_total = row_top + jnp.log(row_total)
        probs = jnp.exp(masked - log_total)
        weights = probs.astype(jnp.bfloat16)
        attended = jnp.dot(weights, value, preferred_element_type=jnp.float32).astype(
            jnp.bfloat16
        )
        row_delta = jnp.sum(
            grad.astype(jnp.float32) * attended.astype(jnp.float32), axis=1, keepdims=True
        )
        dprob = lax.dot_general(grad, value, contract_last, preferred_element_type=jnp.float32)
        dscore = (probs * (dprob - row_delta)).astype(jnp.bfloat16)
        dquery = jnp.dot(dscore, key, preferred_element_type=jnp.float32) * score_scale
        dkey = (
            lax.dot_general(dscore, query, contract_first, preferred_element_type=jnp.float32)
            * score_scale
        )
        dvalue = lax.dot_general(weights, grad, contract_first, preferred_element_type=jnp.float32)
        msg_ref[0, :, side] = dkey[:rows].astype(jnp.bfloat16)
        msg_ref[0, :, value_side] = dvalue[:rows].astype(jnp.bfloat16)
        dk_ref[0, :, side] = dkey[rows:]
        dv_ref[0, :, side] = dvalue[rows:]
        sink_share = jnp.exp(sink - log_total) * row_delta
        for h in range(GROUP):
            part = slice(h * rows, (h + 1) * rows)
            o_ref[0, :, heads[h]] = attended[part]
            dq_ref[0, :, heads[h]] = dquery[part].astype(jnp.bfloat16)
            total = -jnp.sum(sink_share[part], axis=0, keepdims=True)
            st_ref[0, group, pl.ds(h, 1), :] = jnp.broadcast_to(total, (1, 128))


def attend_blocks(sink_logit, queries, out_grad, own_pair, prev_pair, allowed):
    lanes, rows, query_width = queries.shape
    pair_width = own_pair.shape[2]
    side_width = KV_HEADS * HEAD_DIM
    lane_block = lambda width: pl.BlockSpec((1, rows, width), lambda lane: (lane, 0, 0))
    flops = 2 * lanes * HEADS * rows * 2 * rows * HEAD_DIM * 6
    moved = 8 * queries.size + 4 * own_pair.size + 6 * own_pair.size + 4 * allowed.size
    return pl.pallas_call(
        group_kernel,
        grid=(lanes,),
        in_specs=[
            pl.BlockSpec(memory_space=pltpu.SMEM),
            lane_block(query_width),
            lane_block(query_width),
            lane_block(pair_width),
            lane_block(pair_width),
            pl.BlockSpec((1, rows, 2 * rows), lambda lane: (lane, 0, 0)),
        ],
        out_specs=[
            lane_block(query_width),
            lane_block(query_width),
            lane_block(pair_width),
            lane_block(side_width),
            lane_block(side_width),
            pl.BlockSpec((1, KV_HEADS, GROUP, 128), lambda lane: (lane, 0, 0, 0)),
        ],
        out_shape=[
            jax.ShapeDtypeStruct((lanes, rows, query_width), jnp.bfloat16),
            jax.ShapeDtypeStruct((lanes, rows, query_width), jnp.bfloat16),
            jax.ShapeDtypeStruct((lanes, rows, pair_width), jnp.bfloat16),
            jax.ShapeDtypeStruct((lanes, rows, side_width), jnp.float32),
            jax.ShapeDtypeStruct((lanes, rows, side_width), jnp.float32),
            jax.ShapeDtypeStruct((lanes, KV_HEADS, GROUP, 128), jnp.float32),
        ],
        cost_estimate=pl.CostEstimate(
            flops=flops, transcendentals=4 * lanes * HEADS * rows * rows, bytes_accessed=moved
        ),
    )(sink_logit, queries, out_grad, own_pair, prev_pair, allowed)


def per_device(queries, keys, values, doc_bounds, sink_logit, out_grad):
    block_rows = queries.shape[3]
    query_width = queries.shape[4]
    value_width = keys.shape[4]
    pair_count = lax.axis_size("ctx")
    my_index = lax.axis_index("ctx")
    score_scale = 1.0 / math.sqrt(HEAD_DIM)
    at_fold = my_index == pair_count - 1
    last_block = 2 * pair_count - 1
    span = (REACH + 1) * block_rows

    own_pair = jnp.concatenate(
        [keys.reshape(2, block_rows, value_width), values.reshape(2, block_rows, value_width)], axis=2
    )
    prev0, prev1 = neighbour_swap(own_pair[0], own_pair[1], "ctx")
    prev1 = jnp.where(at_fold, own_pair[0], prev1)
    prev_pair = jnp.stack([prev0, prev1])

    lane_block = jnp.stack([my_index, last_block - my_index]).astype(jnp.int32)
    row_offsets = jnp.arange(block_rows, dtype=jnp.int32)
    window_offsets = jnp.arange(span, dtype=jnp.int32)
    query_pos = lane_block[:, None] * block_rows + row_offsets[None, :]
    key_pos = (lane_block[:, None] - REACH) * block_rows + window_offsets[None, :]
    first_pos = doc_bounds.reshape(2, 2, block_rows)[:, 0]
    allowed = (key_pos[:, None, :] <= query_pos[:, :, None]) & (
        key_pos[:, None, :] >= first_pos[:, :, None]
    )
    attended, dquery, message, key_own, value_own, sink_parts = attend_blocks(
        sink_logit,
        queries.reshape(2, block_rows, query_width),
        out_grad.reshape(2, block_rows, query_width),
        own_pair,
        prev_pair,
        allowed.astype(jnp.float32),
    )
    sink_terms = jnp.sum(sink_parts[:, :, :, 0], axis=0)
    sink_grad = all_sum(sink_terms.reshape(HEADS), ("ctx", "dp"))

    into1, into0 = neighbour_swap(message[1], message[0], "ctx")
    into0 = jnp.where(at_fold, message[1], into0)
    arrived = jnp.stack([into0, into1]).astype(jnp.float32)

    out_shape = (1, 1, 2, block_rows, query_width)
    pair_out = (1, 1, 2, block_rows, value_width)
    attn_out = attended.reshape(out_shape)
    query_grad = dquery.reshape(out_shape)
    key_grad = (key_own + arrived[:, :, :value_width]).astype(jnp.bfloat16).reshape(pair_out)
    value_grad = (value_own + arrived[:, :, value_width:]).astype(jnp.bfloat16).reshape(pair_out)
    return (attn_out, query_grad, key_grad, value_grad, sink_grad)


def solution(mesh):
    in_specs = (
        P("dp", "ctx", None, None, None),
        P("dp", "ctx", None, None, None),
        P("dp", "ctx", None, None, None),
        P("dp", "ctx", None, None, None),
        P(),
        P("dp", "ctx", None, None, None),
    )
    out_specs = (
        P("dp", "ctx", None, None, None),
        P("dp", "ctx", None, None, None),
        P("dp", "ctx", None, None, None),
        P("dp", "ctx", None, None, None),
        P(),
    )
    return jax.shard_map(
        per_device, mesh=mesh, in_specs=in_specs, out_specs=out_specs, check_vma=False
    )
```

```python
import math

import jax
import jax.numpy as jnp
from jax import lax
from jax.experimental import pallas as pl
from jax.experimental.pallas import tpu as pltpu
from jax.sharding import PartitionSpec as P

HEADS = 32
KV_HEADS = 4
HEAD_DIM = 128
GROUP = 8
REACH = 1


def shift_up(x, axis):
    size = lax.axis_size(axis)
    return lax.ppermute(x, axis, [(i, i + 1) for i in range(size - 1)])


def shift_down(x, axis):
    size = lax.axis_size(axis)
    return lax.ppermute(x, axis, [(i + 1, i) for i in range(size - 1)])


def swap_pairs(x, axis, offset):
    size = lax.axis_size(axis)
    pairs = []
    for i in range(size):
        partner = i + 1 if (i - offset) % 2 == 0 else i - 1
        if partner == size:
            partner = i
        if partner >= 0:
            pairs.append((i, partner))
    return lax.ppermute(x, axis, pairs)


def all_sum(x, axes):
    count = 1
    for axis in axes:
        count *= lax.axis_size(axis)
    spread = jnp.broadcast_to(x[None], (count,) + x.shape)
    return jnp.sum(lax.all_to_all(spread, axes, 0, 0, tiled=True), axis=0)


def group_kernel(
    flag_ref, sink_ref, q_ref, g_ref, k_ref, v_ref, first_ref, second_ref, allow_ref,
    o_ref, dq_ref, msg_ref, dk_ref, dv_ref, st_ref,
):
    rows = q_ref.shape[1]
    score_scale = 1.0 / math.sqrt(HEAD_DIM)
    contract_last = (((1,), (1,)), ((), ()))
    contract_first = (((0,), (0,)), ((), ()))
    allowed = jnp.concatenate([allow_ref[0]] * GROUP, axis=0) > 0.5
    head_of_row = lax.broadcasted_iota(jnp.int32, (GROUP * rows, 1), 0) // rows
    use_second = (pl.program_id(0) + flag_ref[0]) % 2 == 1
    for group in range(KV_HEADS):
        heads = [pl.ds((group * GROUP + h) * HEAD_DIM, HEAD_DIM) for h in range(GROUP)]
        side = pl.ds(group * HEAD_DIM, HEAD_DIM)
        value_side = pl.ds((KV_HEADS + group) * HEAD_DIM, HEAD_DIM)
        query = jnp.concatenate([q_ref[0, :, cols] for cols in heads], axis=0)
        grad = jnp.concatenate([g_ref[0, :, cols] for cols in heads], axis=0)
        prev_key = jnp.where(use_second, second_ref[:, side], first_ref[:, side])
        prev_value = jnp.where(use_second, second_ref[:, value_side], first_ref[:, value_side])
        key = jnp.concatenate([prev_key, k_ref[0, :, side]], axis=0)
        value = jnp.concatenate([prev_value, v_ref[0, :, side]], axis=0)
        sink = jnp.zeros((GROUP * rows, 1), jnp.float32)
        for h in range(GROUP):
            sink = jnp.where(head_of_row == h, sink_ref[group * GROUP + h], sink)
        scores = (
            lax.dot_general(query, key, contract_last, preferred_element_type=jnp.float32)
            * score_scale
        )
        masked = jnp.where(allowed, scores, -jnp.inf)
        row_top = jnp.maximum(sink, jnp.max(masked, axis=1, keepdims=True))
        row_total = jnp.exp(sink - row_top) + jnp.sum(
            jnp.exp(masked - row_top), axis=1, keepdims=True
        )
        log_total = row_top + jnp.log(row_total)
        probs = jnp.exp(masked - log_total)
        weights = probs.astype(jnp.bfloat16)
        attended = jnp.dot(weights, value, preferred_element_type=jnp.float32).astype(
            jnp.bfloat16
        )
        row_delta = jnp.sum(
            grad.astype(jnp.float32) * attended.astype(jnp.float32), axis=1, keepdims=True
        )
        dprob = lax.dot_general(grad, value, contract_last, preferred_element_type=jnp.float32)
        dscore = (probs * (dprob - row_delta)).astype(jnp.bfloat16)
        dquery = jnp.dot(dscore, key, preferred_element_type=jnp.float32) * score_scale
        dkey = (
            lax.dot_general(dscore, query, contract_first, preferred_element_type=jnp.float32)
            * score_scale
        )
        dvalue = lax.dot_general(weights, grad, contract_first, preferred_element_type=jnp.float32)
        msg_ref[0, :, side] = dkey[:rows].astype(jnp.bfloat16)
        msg_ref[0, :, value_side] = dvalue[:rows].astype(jnp.bfloat16)
        dk_ref[0, :, side] = dkey[rows:]
        dv_ref[0, :, side] = dvalue[rows:]
        sink_share = jnp.exp(sink - log_total) * row_delta
        for h in range(GROUP):
            part = slice(h * rows, (h + 1) * rows)
            o_ref[0, :, heads[h]] = attended[part]
            dq_ref[0, :, heads[h]] = dquery[part].astype(jnp.bfloat16)
            total = -jnp.sum(sink_share[part], axis=0, keepdims=True)
            st_ref[0, group, pl.ds(h, 1), :] = jnp.broadcast_to(total, (1, 128))


def attend_blocks(flag, sink_logit, queries, out_grad, keys, values, first, second, allowed):
    lanes, rows, query_width = queries.shape
    side_width = keys.shape[2]
    pair_width = first.shape[1]
    lane_block = lambda width: pl.BlockSpec((1, rows, width), lambda lane, flag_ref: (lane, 0, 0))
    whole = pl.BlockSpec((rows, pair_width), lambda lane, flag_ref: (0, 0))
    flops = 2 * lanes * HEADS * rows * 2 * rows * HEAD_DIM * 6
    moved = 8 * queries.size + 4 * keys.size + 10 * keys.size + 4 * allowed.size
    grid_spec = pltpu.PrefetchScalarGridSpec(
        num_scalar_prefetch=1,
        grid=(lanes,),
        in_specs=[
            pl.BlockSpec(memory_space=pltpu.SMEM),
            lane_block(query_width),
            lane_block(query_width),
            lane_block(side_width),
            lane_block(side_width),
            whole,
            whole,
            pl.BlockSpec((1, rows, 2 * rows), lambda lane, flag_ref: (lane, 0, 0)),
        ],
        out_specs=[
            lane_block(query_width),
            lane_block(query_width),
            pl.BlockSpec(
                (1, rows, pair_width), lambda lane, flag_ref: ((lane + flag_ref[0]) % 2, 0, 0)
            ),
            lane_block(side_width),
            lane_block(side_width),
            pl.BlockSpec((1, KV_HEADS, GROUP, 128), lambda lane, flag_ref: (lane, 0, 0, 0)),
        ],
    )
    return pl.pallas_call(
        group_kernel,
        grid_spec=grid_spec,
        out_shape=[
            jax.ShapeDtypeStruct((lanes, rows, query_width), jnp.bfloat16),
            jax.ShapeDtypeStruct((lanes, rows, query_width), jnp.bfloat16),
            jax.ShapeDtypeStruct((lanes, rows, pair_width), jnp.bfloat16),
            jax.ShapeDtypeStruct((lanes, rows, side_width), jnp.float32),
            jax.ShapeDtypeStruct((lanes, rows, side_width), jnp.float32),
            jax.ShapeDtypeStruct((lanes, KV_HEADS, GROUP, 128), jnp.float32),
        ],
        cost_estimate=pl.CostEstimate(
            flops=flops, transcendentals=4 * lanes * HEADS * rows * rows, bytes_accessed=moved
        ),
    )(flag, sink_logit, queries, out_grad, keys, values, first, second, allowed)


def per_device(queries, keys, values, doc_bounds, sink_logit, out_grad):
    block_rows = queries.shape[3]
    query_width = queries.shape[4]
    value_width = keys.shape[4]
    pair_count = lax.axis_size("ctx")
    my_index = lax.axis_index("ctx")
    score_scale = 1.0 / math.sqrt(HEAD_DIM)
    last_block = 2 * pair_count - 1
    span = (REACH + 1) * block_rows

    key_lanes = keys.reshape(2, block_rows, value_width)
    value_lanes = values.reshape(2, block_rows, value_width)
    even = (my_index % 2 == 0).astype(jnp.int32)

    def lane_pair(lane):
        return jnp.concatenate(
            [
                lax.dynamic_index_in_dim(key_lanes, lane, keepdims=False),
                lax.dynamic_index_in_dim(value_lanes, lane, keepdims=False),
            ],
            axis=1,
        )

    first_send, second_send = lax.optimization_barrier((lane_pair(1 - even), lane_pair(even)))
    first = swap_pairs(first_send, "ctx", 0)
    second = swap_pairs(second_send, "ctx", 1)

    lane_block = jnp.stack([my_index, last_block - my_index]).astype(jnp.int32)
    row_offsets = jnp.arange(block_rows, dtype=jnp.int32)
    window_offsets = jnp.arange(span, dtype=jnp.int32)
    query_pos = lane_block[:, None] * block_rows + row_offsets[None, :]
    key_pos = (lane_block[:, None] - REACH) * block_rows + window_offsets[None, :]
    first_pos = doc_bounds.reshape(2, 2, block_rows)[:, 0]
    allowed = (key_pos[:, None, :] <= query_pos[:, :, None]) & (
        key_pos[:, None, :] >= first_pos[:, :, None]
    )
    attended, dquery, message, key_own, value_own, sink_parts = attend_blocks(
        even.reshape(1),
        sink_logit,
        queries.reshape(2, block_rows, query_width),
        out_grad.reshape(2, block_rows, query_width),
        key_lanes,
        value_lanes,
        first,
        second,
        allowed.astype(jnp.float32),
    )
    sink_terms = jnp.sum(sink_parts[:, :, :, 0], axis=0)
    sink_grad = all_sum(sink_terms.reshape(HEADS), ("ctx", "dp"))

    sent_first, sent_second = lax.optimization_barrier((message[0], message[1]))
    got_first = swap_pairs(sent_first, "ctx", 0)
    got_second = swap_pairs(sent_second, "ctx", 1)
    is_even = even == 1
    arrived = jnp.stack(
        [jnp.where(is_even, got_first, got_second), jnp.where(is_even, got_second, got_first)]
    ).astype(jnp.float32)

    out_shape = (1, 1, 2, block_rows, query_width)
    pair_out = (1, 1, 2, block_rows, value_width)
    attn_out = attended.reshape(out_shape)
    query_grad = dquery.reshape(out_shape)
    key_grad = (key_own + arrived[:, :, :value_width]).astype(jnp.bfloat16).reshape(pair_out)
    value_grad = (value_own + arrived[:, :, value_width:]).astype(jnp.bfloat16).reshape(pair_out)
    return (attn_out, query_grad, key_grad, value_grad, sink_grad)


def solution(mesh):
    in_specs = (
        P("dp", "ctx", None, None, None),
        P("dp", "ctx", None, None, None),
        P("dp", "ctx", None, None, None),
        P("dp", "ctx", None, None, None),
        P(),
        P("dp", "ctx", None, None, None),
    )
    out_specs = (
        P("dp", "ctx", None, None, None),
        P("dp", "ctx", None, None, None),
        P("dp", "ctx", None, None, None),
        P("dp", "ctx", None, None, None),
        P(),
    )
    return jax.shard_map(
        per_device, mesh=mesh, in_specs=in_specs, out_specs=out_specs, check_vma=False
    )
```

```python
import math

import jax
import jax.numpy as jnp
from jax import lax
from jax.experimental import pallas as pl
from jax.experimental.pallas import tpu as pltpu
from jax.sharding import PartitionSpec as P

HEADS = 32
KV_HEADS = 4
HEAD_DIM = 128
GROUP = 8
REACH = 1


def shift_up(x, axis):
    size = lax.axis_size(axis)
    return lax.ppermute(x, axis, [(i, i + 1) for i in range(size - 1)])


def shift_down(x, axis):
    size = lax.axis_size(axis)
    return lax.ppermute(x, axis, [(i + 1, i) for i in range(size - 1)])


def swap_pairs(x, axis, offset):
    size = lax.axis_size(axis)
    pairs = []
    for i in range(size):
        partner = i + 1 if (i - offset) % 2 == 0 else i - 1
        if partner == size:
            partner = i
        if partner >= 0:
            pairs.append((i, partner))
    return lax.ppermute(x, axis, pairs)


def all_sum(spread, axes):
    return jnp.sum(lax.all_to_all(spread, axes, 0, 0, tiled=True), axis=0)


def group_kernel(
    flag_ref, sink_ref, q_ref, g_ref, k_ref, v_ref, first_ref, second_ref, allow_ref,
    o_ref, dq_ref, first_msg_ref, second_msg_ref, dk_ref, dv_ref, st_ref,
):
    rows = q_ref.shape[1]
    score_scale = 1.0 / math.sqrt(HEAD_DIM)
    contract_last = (((1,), (1,)), ((), ()))
    contract_first = (((0,), (0,)), ((), ()))
    allowed = jnp.concatenate([allow_ref[0]] * GROUP, axis=0) > 0.5
    head_of_row = lax.broadcasted_iota(jnp.int32, (GROUP * rows, 1), 0) // rows
    use_second = (pl.program_id(0) + flag_ref[0]) % 2 == 1
    head_lane = lax.broadcasted_iota(jnp.int32, (1, HEADS), 1)
    sink_row = jnp.zeros((1, HEADS), jnp.float32)
    for group in range(KV_HEADS):
        heads = [pl.ds((group * GROUP + h) * HEAD_DIM, HEAD_DIM) for h in range(GROUP)]
        side = pl.ds(group * HEAD_DIM, HEAD_DIM)
        value_side = pl.ds((KV_HEADS + group) * HEAD_DIM, HEAD_DIM)
        query = jnp.concatenate([q_ref[0, :, cols] for cols in heads], axis=0)
        grad = jnp.concatenate([g_ref[0, :, cols] for cols in heads], axis=0)
        prev_key = jnp.where(use_second, second_ref[:, side], first_ref[:, side])
        prev_value = jnp.where(use_second, second_ref[:, value_side], first_ref[:, value_side])
        key = jnp.concatenate([prev_key, k_ref[0, :, side]], axis=0)
        value = jnp.concatenate([prev_value, v_ref[0, :, side]], axis=0)
        sink = jnp.zeros((GROUP * rows, 1), jnp.float32)
        for h in range(GROUP):
            sink = jnp.where(head_of_row == h, sink_ref[group * GROUP + h], sink)
        scores = (
            lax.dot_general(query, key, contract_last, preferred_element_type=jnp.float32)
            * score_scale
        )
        masked = jnp.where(allowed, scores, -jnp.inf)
        row_top = jnp.maximum(sink, jnp.max(masked, axis=1, keepdims=True))
        row_total = jnp.exp(sink - row_top) + jnp.sum(
            jnp.exp(masked - row_top), axis=1, keepdims=True
        )
        log_total = row_top + jnp.log(row_total)
        probs = jnp.exp(masked - log_total)
        weights = probs.astype(jnp.bfloat16)
        attended = jnp.dot(weights, value, preferred_element_type=jnp.float32).astype(
            jnp.bfloat16
        )
        row_delta = jnp.sum(
            grad.astype(jnp.float32) * attended.astype(jnp.float32), axis=1, keepdims=True
        )
        dprob = lax.dot_general(grad, value, contract_last, preferred_element_type=jnp.float32)
        dscore = (probs * (dprob - row_delta)).astype(jnp.bfloat16)
        dquery = jnp.dot(dscore, key, preferred_element_type=jnp.float32) * score_scale
        dkey = (
            lax.dot_general(dscore, query, contract_first, preferred_element_type=jnp.float32)
            * score_scale
        )
        dvalue = lax.dot_general(weights, grad, contract_first, preferred_element_type=jnp.float32)
        for msg_ref, slot in ((first_msg_ref, 0), (second_msg_ref, 1)):

            @pl.when((pl.program_id(0) + flag_ref[0]) % 2 == slot)
            def _():
                msg_ref[:, side] = dkey[:rows].astype(jnp.bfloat16)
                msg_ref[:, value_side] = dvalue[:rows].astype(jnp.bfloat16)

        dk_ref[0, :, side] = dkey[rows:]
        dv_ref[0, :, side] = dvalue[rows:]
        sink_share = jnp.exp(sink - log_total) * row_delta
        for h in range(GROUP):
            part = slice(h * rows, (h + 1) * rows)
            o_ref[0, :, heads[h]] = attended[part]
            dq_ref[0, :, heads[h]] = dquery[part].astype(jnp.bfloat16)
            total = -jnp.sum(sink_share[part], axis=0, keepdims=True)
            sink_row = jnp.where(head_lane == group * GROUP + h, total, sink_row)

    @pl.when(pl.program_id(0) == 0)
    def _():
        st_ref[...] = jnp.zeros_like(st_ref)

    st_ref[...] += jnp.broadcast_to(sink_row, st_ref.shape)


def attend_blocks(
    flag, sink_logit, queries, out_grad, keys, values, first, second, allowed, devices
):
    lanes, rows, query_width = queries.shape
    side_width = keys.shape[2]
    pair_width = first.shape[1]
    lane_block = lambda width: pl.BlockSpec((1, rows, width), lambda lane, flag_ref: (lane, 0, 0))
    whole = pl.BlockSpec((rows, pair_width), lambda lane, flag_ref: (0, 0))
    flops = 2 * lanes * HEADS * rows * 2 * rows * HEAD_DIM * 6
    moved = 8 * queries.size + 4 * keys.size + 10 * keys.size + 4 * allowed.size
    grid_spec = pltpu.PrefetchScalarGridSpec(
        num_scalar_prefetch=1,
        grid=(lanes,),
        in_specs=[
            pl.BlockSpec(memory_space=pltpu.SMEM),
            lane_block(query_width),
            lane_block(query_width),
            lane_block(side_width),
            lane_block(side_width),
            whole,
            whole,
            pl.BlockSpec((1, rows, 2 * rows), lambda lane, flag_ref: (lane, 0, 0)),
        ],
        out_specs=[
            lane_block(query_width),
            lane_block(query_width),
            whole,
            whole,
            lane_block(side_width),
            lane_block(side_width),
            pl.BlockSpec((devices, HEADS), lambda lane, flag_ref: (0, 0)),
        ],
    )
    return pl.pallas_call(
        group_kernel,
        grid_spec=grid_spec,
        out_shape=[
            jax.ShapeDtypeStruct((lanes, rows, query_width), jnp.bfloat16),
            jax.ShapeDtypeStruct((lanes, rows, query_width), jnp.bfloat16),
            jax.ShapeDtypeStruct((rows, pair_width), jnp.bfloat16),
            jax.ShapeDtypeStruct((rows, pair_width), jnp.bfloat16),
            jax.ShapeDtypeStruct((lanes, rows, side_width), jnp.float32),
            jax.ShapeDtypeStruct((lanes, rows, side_width), jnp.float32),
            jax.ShapeDtypeStruct((devices, HEADS), jnp.float32),
        ],
        cost_estimate=pl.CostEstimate(
            flops=flops, transcendentals=4 * lanes * HEADS * rows * rows, bytes_accessed=moved
        ),
    )(flag, sink_logit, queries, out_grad, keys, values, first, second, allowed)


def per_device(queries, keys, values, doc_bounds, sink_logit, out_grad):
    block_rows = queries.shape[3]
    query_width = queries.shape[4]
    value_width = keys.shape[4]
    pair_count = lax.axis_size("ctx")
    my_index = lax.axis_index("ctx")
    score_scale = 1.0 / math.sqrt(HEAD_DIM)
    last_block = 2 * pair_count - 1
    span = (REACH + 1) * block_rows

    key_lanes = keys.reshape(2, block_rows, value_width)
    value_lanes = values.reshape(2, block_rows, value_width)
    even = (my_index % 2 == 0).astype(jnp.int32)

    def lane_pair(lane):
        return jnp.concatenate(
            [
                lax.dynamic_index_in_dim(key_lanes, lane, keepdims=False),
                lax.dynamic_index_in_dim(value_lanes, lane, keepdims=False),
            ],
            axis=1,
        )

    first_send, second_send = lax.optimization_barrier((lane_pair(1 - even), lane_pair(even)))
    first = swap_pairs(first_send, "ctx", 0)
    second = swap_pairs(second_send, "ctx", 1)

    lane_block = jnp.stack([my_index, last_block - my_index]).astype(jnp.int32)
    row_offsets = jnp.arange(block_rows, dtype=jnp.int32)
    window_offsets = jnp.arange(span, dtype=jnp.int32)
    query_pos = lane_block[:, None] * block_rows + row_offsets[None, :]
    key_pos = (lane_block[:, None] - REACH) * block_rows + window_offsets[None, :]
    first_pos = doc_bounds.reshape(2, 2, block_rows)[:, 0]
    allowed = (key_pos[:, None, :] <= query_pos[:, :, None]) & (
        key_pos[:, None, :] >= first_pos[:, :, None]
    )
    devices = lax.axis_size("ctx") * lax.axis_size("dp")
    attended, dquery, sent_first, sent_second, key_own, value_own, sink_spread = attend_blocks(
        even.reshape(1),
        sink_logit,
        queries.reshape(2, block_rows, query_width),
        out_grad.reshape(2, block_rows, query_width),
        key_lanes,
        value_lanes,
        first,
        second,
        allowed.astype(jnp.float32),
        devices,
    )
    sink_grad = all_sum(sink_spread, ("ctx", "dp"))

    got_first = swap_pairs(sent_first, "ctx", 0)
    got_second = swap_pairs(sent_second, "ctx", 1)
    is_even = even == 1
    arrived = jnp.stack(
        [jnp.where(is_even, got_first, got_second), jnp.where(is_even, got_second, got_first)]
    ).astype(jnp.float32)

    out_shape = (1, 1, 2, block_rows, query_width)
    pair_out = (1, 1, 2, block_rows, value_width)
    attn_out = attended.reshape(out_shape)
    query_grad = dquery.reshape(out_shape)
    key_grad = (key_own + arrived[:, :, :value_width]).astype(jnp.bfloat16).reshape(pair_out)
    value_grad = (value_own + arrived[:, :, value_width:]).astype(jnp.bfloat16).reshape(pair_out)
    return (attn_out, query_grad, key_grad, value_grad, sink_grad)


def solution(mesh):
    in_specs = (
        P("dp", "ctx", None, None, None),
        P("dp", "ctx", None, None, None),
        P("dp", "ctx", None, None, None),
        P("dp", "ctx", None, None, None),
        P(),
        P("dp", "ctx", None, None, None),
    )
    out_specs = (
        P("dp", "ctx", None, None, None),
        P("dp", "ctx", None, None, None),
        P("dp", "ctx", None, None, None),
        P("dp", "ctx", None, None, None),
        P(),
    )
    return jax.shard_map(
        per_device, mesh=mesh, in_specs=in_specs, out_specs=out_specs, check_vma=False
    )
```

```python
import math

import jax
import jax.numpy as jnp
from jax import lax
from jax.experimental import pallas as pl
from jax.experimental.pallas import tpu as pltpu
from jax.sharding import PartitionSpec as P

HEADS = 32
KV_HEADS = 4
HEAD_DIM = 128
GROUP = 8
REACH = 1


def shift_up(x, axis):
    size = lax.axis_size(axis)
    return lax.ppermute(x, axis, [(i, i + 1) for i in range(size - 1)])


def shift_down(x, axis):
    size = lax.axis_size(axis)
    return lax.ppermute(x, axis, [(i + 1, i) for i in range(size - 1)])


def swap_pairs(x, axis, offset):
    size = lax.axis_size(axis)
    pairs = []
    for i in range(size):
        partner = i + 1 if (i - offset) % 2 == 0 else i - 1
        if partner == size:
            partner = i
        if partner >= 0:
            pairs.append((i, partner))
    return lax.ppermute(x, axis, pairs)


def all_sum(spread, axes):
    return jnp.sum(lax.all_to_all(spread, axes, 0, 0, tiled=True), axis=0)


def group_kernel(
    flag_ref, sink_ref, q_ref, g_ref, k_ref, v_ref, first_ref, second_ref, allow_ref,
    o_ref, dq_ref, first_msg_ref, second_msg_ref, dk_ref, dv_ref, st_ref,
):
    rows = q_ref.shape[1]
    score_scale = 1.0 / math.sqrt(HEAD_DIM)
    contract_last = (((1,), (1,)), ((), ()))
    contract_first = (((0,), (0,)), ((), ()))
    allowed = jnp.concatenate([allow_ref[0]] * GROUP, axis=0) > 0.5
    head_of_row = lax.broadcasted_iota(jnp.int32, (GROUP * rows, 1), 0) // rows
    use_second = (pl.program_id(0) + flag_ref[0]) % 2 == 1
    head_lane = lax.broadcasted_iota(jnp.int32, (1, HEADS), 1)
    sink_row = jnp.zeros((1, HEADS), jnp.float32)
    for group in range(KV_HEADS):
        heads = [pl.ds((group * GROUP + h) * HEAD_DIM, HEAD_DIM) for h in range(GROUP)]
        side = pl.ds(group * HEAD_DIM, HEAD_DIM)
        value_side = pl.ds((KV_HEADS + group) * HEAD_DIM, HEAD_DIM)
        query = jnp.concatenate([q_ref[0, :, cols] for cols in heads], axis=0)
        grad = jnp.concatenate([g_ref[0, :, cols] for cols in heads], axis=0)
        prev_key = jnp.where(use_second, second_ref[:, side], first_ref[:, side])
        prev_value = jnp.where(use_second, second_ref[:, value_side], first_ref[:, value_side])
        key = jnp.concatenate([prev_key, k_ref[0, :, side]], axis=0)
        value = jnp.concatenate([prev_value, v_ref[0, :, side]], axis=0)
        sink = jnp.zeros((GROUP * rows, 1), jnp.float32)
        for h in range(GROUP):
            sink = jnp.where(head_of_row == h, sink_ref[group * GROUP + h], sink)
        scores = (
            lax.dot_general(query, key, contract_last, preferred_element_type=jnp.float32)
            * score_scale
        )
        masked = jnp.where(allowed, scores, -jnp.inf)
        row_top = jnp.maximum(sink, jnp.max(masked, axis=1, keepdims=True))
        row_total = jnp.exp(sink - row_top) + jnp.sum(
            jnp.exp(masked - row_top), axis=1, keepdims=True
        )
        log_total = row_top + jnp.log(row_total)
        probs = jnp.exp(masked - log_total)
        weights = probs.astype(jnp.bfloat16)
        attended = jnp.dot(weights, value, preferred_element_type=jnp.float32).astype(
            jnp.bfloat16
        )
        row_delta = jnp.sum(
            grad.astype(jnp.float32) * attended.astype(jnp.float32), axis=1, keepdims=True
        )
        dprob = lax.dot_general(grad, value, contract_last, preferred_element_type=jnp.float32)
        dscore = (probs * (dprob - row_delta)).astype(jnp.bfloat16)
        dquery = jnp.dot(dscore, key, preferred_element_type=jnp.float32) * score_scale
        dkey = (
            lax.dot_general(dscore, query, contract_first, preferred_element_type=jnp.float32)
            * score_scale
        )
        dvalue = lax.dot_general(weights, grad, contract_first, preferred_element_type=jnp.float32)
        for msg_ref, slot in ((first_msg_ref, 0), (second_msg_ref, 1)):

            @pl.when((pl.program_id(0) + flag_ref[0]) % 2 == slot)
            def _():
                msg_ref[:, side] = dkey[:rows].astype(jnp.bfloat16)
                msg_ref[:, value_side] = dvalue[:rows].astype(jnp.bfloat16)

        dk_ref[0, :, side] = dkey[rows:]
        dv_ref[0, :, side] = dvalue[rows:]
        sink_share = jnp.exp(sink - log_total) * row_delta
        for h in range(GROUP):
            part = slice(h * rows, (h + 1) * rows)
            o_ref[0, :, heads[h]] = attended[part]
            dq_ref[0, :, heads[h]] = dquery[part].astype(jnp.bfloat16)
            total = -jnp.sum(sink_share[part], axis=0, keepdims=True)
            sink_row = jnp.where(head_lane == group * GROUP + h, total, sink_row)

    @pl.when(pl.program_id(0) == 0)
    def _():
        st_ref[...] = jnp.zeros_like(st_ref)

    st_ref[...] += jnp.broadcast_to(sink_row, st_ref.shape)


def attend_blocks(
    flag, sink_logit, queries, out_grad, keys, values, first, second, allowed, devices
):
    lanes, rows, query_width = queries.shape
    side_width = keys.shape[2]
    pair_width = first.shape[1]
    lane_block = lambda width: pl.BlockSpec((1, rows, width), lambda lane, flag_ref: (lane, 0, 0))
    whole = pl.BlockSpec((rows, pair_width), lambda lane, flag_ref: (0, 0))
    flops = 2 * lanes * HEADS * rows * 2 * rows * HEAD_DIM * 6
    moved = 8 * queries.size + 4 * keys.size + 10 * keys.size + 4 * allowed.size
    grid_spec = pltpu.PrefetchScalarGridSpec(
        num_scalar_prefetch=1,
        grid=(lanes,),
        in_specs=[
            pl.BlockSpec(memory_space=pltpu.SMEM),
            lane_block(query_width),
            lane_block(query_width),
            lane_block(side_width),
            lane_block(side_width),
            whole,
            whole,
            pl.BlockSpec((1, rows, 2 * rows), lambda lane, flag_ref: (lane, 0, 0)),
        ],
        out_specs=[
            lane_block(query_width),
            lane_block(query_width),
            whole,
            whole,
            lane_block(side_width),
            lane_block(side_width),
            pl.BlockSpec((devices, HEADS), lambda lane, flag_ref: (0, 0)),
        ],
    )
    return pl.pallas_call(
        group_kernel,
        grid_spec=grid_spec,
        out_shape=[
            jax.ShapeDtypeStruct((lanes, rows, query_width), jnp.bfloat16),
            jax.ShapeDtypeStruct((lanes, rows, query_width), jnp.bfloat16),
            jax.ShapeDtypeStruct((rows, pair_width), jnp.bfloat16),
            jax.ShapeDtypeStruct((rows, pair_width), jnp.bfloat16),
            jax.ShapeDtypeStruct((lanes, rows, side_width), jnp.float32),
            jax.ShapeDtypeStruct((lanes, rows, side_width), jnp.float32),
            jax.ShapeDtypeStruct((devices, HEADS), jnp.float32),
        ],
        cost_estimate=pl.CostEstimate(
            flops=flops, transcendentals=4 * lanes * HEADS * rows * rows, bytes_accessed=moved
        ),
    )(flag, sink_logit, queries, out_grad, keys, values, first, second, allowed)


def per_device(queries, keys, values, doc_bounds, sink_logit, out_grad):
    block_rows = queries.shape[3]
    query_width = queries.shape[4]
    value_width = keys.shape[4]
    pair_count = lax.axis_size("ctx")
    my_index = lax.axis_index("ctx")
    score_scale = 1.0 / math.sqrt(HEAD_DIM)
    last_block = 2 * pair_count - 1
    span = (REACH + 1) * block_rows

    key_lanes = keys.reshape(2, block_rows, value_width)
    value_lanes = values.reshape(2, block_rows, value_width)
    even = (my_index % 2 == 0).astype(jnp.int32)

    def lane_pair(lane):
        return jnp.concatenate(
            [
                lax.dynamic_index_in_dim(key_lanes, lane, keepdims=False),
                lax.dynamic_index_in_dim(value_lanes, lane, keepdims=False),
            ],
            axis=1,
        )

    first_send, second_send = lax.optimization_barrier((lane_pair(1 - even), lane_pair(even)))
    first = swap_pairs(first_send, "ctx", 0)
    second = swap_pairs(second_send, "ctx", 1)

    lane_block = jnp.stack([my_index, last_block - my_index]).astype(jnp.int32)
    row_offsets = jnp.arange(block_rows, dtype=jnp.int32)
    window_offsets = jnp.arange(span, dtype=jnp.int32)
    query_pos = lane_block[:, None] * block_rows + row_offsets[None, :]
    key_pos = (lane_block[:, None] - REACH) * block_rows + window_offsets[None, :]
    first_pos = doc_bounds.reshape(2, 2, block_rows)[:, 0]
    allowed = (key_pos[:, None, :] <= query_pos[:, :, None]) & (
        key_pos[:, None, :] >= first_pos[:, :, None]
    )
    devices = lax.axis_size("ctx") * lax.axis_size("dp")
    attended, dquery, sent_first, sent_second, key_own, value_own, sink_spread = attend_blocks(
        even.reshape(1),
        sink_logit,
        queries.reshape(2, block_rows, query_width),
        out_grad.reshape(2, block_rows, query_width),
        key_lanes,
        value_lanes,
        first,
        second,
        allowed.astype(jnp.float32),
        devices,
    )
    sink_grad = all_sum(sink_spread, ("ctx", "dp"))

    sent_first, sent_second, sink_grad = lax.optimization_barrier(
        (sent_first, sent_second, sink_grad)
    )
    got_first = swap_pairs(sent_first, "ctx", 0)
    got_second = swap_pairs(sent_second, "ctx", 1)
    is_even = even == 1
    arrived = jnp.stack(
        [jnp.where(is_even, got_first, got_second), jnp.where(is_even, got_second, got_first)]
    ).astype(jnp.float32)

    out_shape = (1, 1, 2, block_rows, query_width)
    pair_out = (1, 1, 2, block_rows, value_width)
    attn_out = attended.reshape(out_shape)
    query_grad = dquery.reshape(out_shape)
    key_grad = (key_own + arrived[:, :, :value_width]).astype(jnp.bfloat16).reshape(pair_out)
    value_grad = (value_own + arrived[:, :, value_width:]).astype(jnp.bfloat16).reshape(pair_out)
    return (attn_out, query_grad, key_grad, value_grad, sink_grad)


def solution(mesh):
    in_specs = (
        P("dp", "ctx", None, None, None),
        P("dp", "ctx", None, None, None),
        P("dp", "ctx", None, None, None),
        P("dp", "ctx", None, None, None),
        P(),
        P("dp", "ctx", None, None, None),
    )
    out_specs = (
        P("dp", "ctx", None, None, None),
        P("dp", "ctx", None, None, None),
        P("dp", "ctx", None, None, None),
        P("dp", "ctx", None, None, None),
        P(),
    )
    return jax.shard_map(
        per_device, mesh=mesh, in_specs=in_specs, out_specs=out_specs, check_vma=False
    )
```

```python
import functools
import math

import jax
import jax.numpy as jnp
from jax import lax
from jax.experimental import pallas as pl
from jax.experimental.pallas import tpu as pltpu
from jax.sharding import PartitionSpec as P

HEADS = 32
KV_HEADS = 4
HEAD_DIM = 128
GROUP = 8
REACH = 1


def shift_up(x, axis):
    size = lax.axis_size(axis)
    return lax.ppermute(x, axis, [(i, i + 1) for i in range(size - 1)])


def shift_down(x, axis):
    size = lax.axis_size(axis)
    return lax.ppermute(x, axis, [(i + 1, i) for i in range(size - 1)])


def swap_pairs(x, axis, offset):
    size = lax.axis_size(axis)
    pairs = []
    for i in range(size):
        partner = i + 1 if (i - offset) % 2 == 0 else i - 1
        if partner == size:
            partner = i
        if partner >= 0:
            pairs.append((i, partner))
    return lax.ppermute(x, axis, pairs)


def all_sum(x, axes):
    count = 1
    for axis in axes:
        count *= lax.axis_size(axis)
    spread = jnp.broadcast_to(x[None], (count,) + x.shape)
    return jnp.sum(lax.all_to_all(spread, axes, 0, 0, tiled=True), axis=0)


def group_kernel(forward, flag_ref, sink_ref, q_ref, g_ref, k_ref, v_ref, first_ref, second_ref,
                 allow_ref, *refs):
    if forward:
        o_ref, st_ref = refs
    else:
        o_ref, dq_ref, msg_ref, dk_ref, dv_ref = refs
    rows = q_ref.shape[1]
    score_scale = 1.0 / math.sqrt(HEAD_DIM)
    contract_last = (((1,), (1,)), ((), ()))
    contract_first = (((0,), (0,)), ((), ()))
    allowed = jnp.concatenate([allow_ref[0]] * GROUP, axis=0) > 0.5
    head_of_row = lax.broadcasted_iota(jnp.int32, (GROUP * rows, 1), 0) // rows
    use_second = (pl.program_id(0) + flag_ref[0]) % 2 == 1
    for group in range(KV_HEADS):
        heads = [pl.ds((group * GROUP + h) * HEAD_DIM, HEAD_DIM) for h in range(GROUP)]
        side = pl.ds(group * HEAD_DIM, HEAD_DIM)
        value_side = pl.ds((KV_HEADS + group) * HEAD_DIM, HEAD_DIM)
        query = jnp.concatenate([q_ref[0, :, cols] for cols in heads], axis=0)
        grad = jnp.concatenate([g_ref[0, :, cols] for cols in heads], axis=0)
        prev_key = jnp.where(use_second, second_ref[:, side], first_ref[:, side])
        prev_value = jnp.where(use_second, second_ref[:, value_side], first_ref[:, value_side])
        key = jnp.concatenate([prev_key, k_ref[0, :, side]], axis=0)
        value = jnp.concatenate([prev_value, v_ref[0, :, side]], axis=0)
        sink = jnp.zeros((GROUP * rows, 1), jnp.float32)
        for h in range(GROUP):
            sink = jnp.where(head_of_row == h, sink_ref[group * GROUP + h], sink)
        scores = (
            lax.dot_general(query, key, contract_last, preferred_element_type=jnp.float32)
            * score_scale
        )
        masked = jnp.where(allowed, scores, -jnp.inf)
        row_top = jnp.maximum(sink, jnp.max(masked, axis=1, keepdims=True))
        row_total = jnp.exp(sink - row_top) + jnp.sum(
            jnp.exp(masked - row_top), axis=1, keepdims=True
        )
        log_total = row_top + jnp.log(row_total)
        probs = jnp.exp(masked - log_total)
        weights = probs.astype(jnp.bfloat16)
        if forward:
            attended = jnp.dot(weights, value, preferred_element_type=jnp.float32).astype(
                jnp.bfloat16
            )
        else:
            attended = jnp.concatenate([o_ref[0, :, cols] for cols in heads], axis=0)
        row_delta = jnp.sum(
            grad.astype(jnp.float32) * attended.astype(jnp.float32), axis=1, keepdims=True
        )
        if forward:
            sink_share = jnp.exp(sink - log_total) * row_delta
            for h in range(GROUP):
                part = slice(h * rows, (h + 1) * rows)
                o_ref[0, :, heads[h]] = attended[part]
                total = -jnp.sum(sink_share[part], axis=0, keepdims=True)
                st_ref[0, group, pl.ds(h, 1), :] = jnp.broadcast_to(total, (1, 128))
            continue
        dprob = lax.dot_general(grad, value, contract_last, preferred_element_type=jnp.float32)
        dscore = (probs * (dprob - row_delta)).astype(jnp.bfloat16)
        dquery = jnp.dot(dscore, key, preferred_element_type=jnp.float32) * score_scale
        dkey = (
            lax.dot_general(dscore, query, contract_first, preferred_element_type=jnp.float32)
            * score_scale
        )
        dvalue = lax.dot_general(weights, grad, contract_first, preferred_element_type=jnp.float32)
        msg_ref[0, :, side] = dkey[:rows].astype(jnp.bfloat16)
        msg_ref[0, :, value_side] = dvalue[:rows].astype(jnp.bfloat16)
        dk_ref[0, :, side] = dkey[rows:]
        dv_ref[0, :, side] = dvalue[rows:]
        for h in range(GROUP):
            part = slice(h * rows, (h + 1) * rows)
            dq_ref[0, :, heads[h]] = dquery[part].astype(jnp.bfloat16)


def attend_blocks(flag, sink_logit, queries, out_grad, keys, values, first, second, allowed,
                  attended=None):
    forward = attended is None
    lanes, rows, query_width = queries.shape
    side_width = keys.shape[2]
    pair_width = first.shape[1]
    lane_block = lambda width: pl.BlockSpec((1, rows, width), lambda lane, flag_ref: (lane, 0, 0))
    whole = pl.BlockSpec((rows, pair_width), lambda lane, flag_ref: (0, 0))
    pass_flops = 2 * lanes * HEADS * rows * 2 * rows * HEAD_DIM
    in_specs = [
        pl.BlockSpec(memory_space=pltpu.SMEM),
        lane_block(query_width),
        lane_block(query_width),
        lane_block(side_width),
        lane_block(side_width),
        whole,
        whole,
        pl.BlockSpec((1, rows, 2 * rows), lambda lane, flag_ref: (lane, 0, 0)),
    ]
    operands = [flag, sink_logit, queries, out_grad, keys, values, first, second, allowed]
    if forward:
        out_specs = [
            lane_block(query_width),
            pl.BlockSpec((1, KV_HEADS, GROUP, 128), lambda lane, flag_ref: (lane, 0, 0, 0)),
        ]
        out_shape = [
            jax.ShapeDtypeStruct((lanes, rows, query_width), jnp.bfloat16),
            jax.ShapeDtypeStruct((lanes, KV_HEADS, GROUP, 128), jnp.float32),
        ]
        flops, moved = 2 * pass_flops, 6 * queries.size + 4 * keys.size + 4 * allowed.size
    else:
        in_specs.append(lane_block(query_width))
        operands.append(attended)
        out_specs = [
            lane_block(query_width),
            pl.BlockSpec(
                (1, rows, pair_width), lambda lane, flag_ref: ((lane + flag_ref[0]) % 2, 0, 0)
            ),
            lane_block(side_width),
            lane_block(side_width),
        ]
        out_shape = [
            jax.ShapeDtypeStruct((lanes, rows, query_width), jnp.bfloat16),
            jax.ShapeDtypeStruct((lanes, rows, pair_width), jnp.bfloat16),
            jax.ShapeDtypeStruct((lanes, rows, side_width), jnp.float32),
            jax.ShapeDtypeStruct((lanes, rows, side_width), jnp.float32),
        ]
        flops, moved = 5 * pass_flops, 8 * queries.size + 12 * keys.size + 4 * allowed.size
    grid_spec = pltpu.PrefetchScalarGridSpec(
        num_scalar_prefetch=1, grid=(lanes,), in_specs=in_specs, out_specs=out_specs
    )
    return pl.pallas_call(
        functools.partial(group_kernel, forward),
        grid_spec=grid_spec,
        out_shape=out_shape,
        cost_estimate=pl.CostEstimate(
            flops=flops, transcendentals=4 * lanes * HEADS * rows * rows, bytes_accessed=moved
        ),
    )(*operands)


def per_device(queries, keys, values, doc_bounds, sink_logit, out_grad):
    block_rows = queries.shape[3]
    query_width = queries.shape[4]
    value_width = keys.shape[4]
    pair_count = lax.axis_size("ctx")
    my_index = lax.axis_index("ctx")
    score_scale = 1.0 / math.sqrt(HEAD_DIM)
    last_block = 2 * pair_count - 1
    span = (REACH + 1) * block_rows

    key_lanes = keys.reshape(2, block_rows, value_width)
    value_lanes = values.reshape(2, block_rows, value_width)
    even = (my_index % 2 == 0).astype(jnp.int32)

    def lane_pair(lane):
        return jnp.concatenate(
            [
                lax.dynamic_index_in_dim(key_lanes, lane, keepdims=False),
                lax.dynamic_index_in_dim(value_lanes, lane, keepdims=False),
            ],
            axis=1,
        )

    first_send, second_send = lax.optimization_barrier((lane_pair(1 - even), lane_pair(even)))
    first = swap_pairs(first_send, "ctx", 0)
    second = swap_pairs(second_send, "ctx", 1)

    lane_block = jnp.stack([my_index, last_block - my_index]).astype(jnp.int32)
    row_offsets = jnp.arange(block_rows, dtype=jnp.int32)
    window_offsets = jnp.arange(span, dtype=jnp.int32)
    query_pos = lane_block[:, None] * block_rows + row_offsets[None, :]
    key_pos = (lane_block[:, None] - REACH) * block_rows + window_offsets[None, :]
    first_pos = doc_bounds.reshape(2, 2, block_rows)[:, 0]
    allowed = (key_pos[:, None, :] <= query_pos[:, :, None]) & (
        key_pos[:, None, :] >= first_pos[:, :, None]
    )
    operands = (
        even.reshape(1),
        sink_logit,
        queries.reshape(2, block_rows, query_width),
        out_grad.reshape(2, block_rows, query_width),
        key_lanes,
        value_lanes,
        first,
        second,
        allowed.astype(jnp.float32),
    )
    attended, sink_parts = attend_blocks(*operands)
    sink_terms = jnp.sum(sink_parts[:, :, :, 0], axis=0)
    sink_grad = all_sum(sink_terms.reshape(HEADS), ("ctx", "dp"))
    dquery, message, key_own, value_own = attend_blocks(*operands, attended)

    sent_first, sent_second, sink_grad = lax.optimization_barrier(
        (message[0], message[1], sink_grad)
    )
    got_first = swap_pairs(sent_first, "ctx", 0)
    got_second = swap_pairs(sent_second, "ctx", 1)
    is_even = even == 1
    arrived = jnp.stack(
        [jnp.where(is_even, got_first, got_second), jnp.where(is_even, got_second, got_first)]
    ).astype(jnp.float32)

    out_shape = (1, 1, 2, block_rows, query_width)
    pair_out = (1, 1, 2, block_rows, value_width)
    attn_out = attended.reshape(out_shape)
    query_grad = dquery.reshape(out_shape)
    key_grad = (key_own + arrived[:, :, :value_width]).astype(jnp.bfloat16).reshape(pair_out)
    value_grad = (value_own + arrived[:, :, value_width:]).astype(jnp.bfloat16).reshape(pair_out)
    return (attn_out, query_grad, key_grad, value_grad, sink_grad)


def solution(mesh):
    in_specs = (
        P("dp", "ctx", None, None, None),
        P("dp", "ctx", None, None, None),
        P("dp", "ctx", None, None, None),
        P("dp", "ctx", None, None, None),
        P(),
        P("dp", "ctx", None, None, None),
    )
    out_specs = (
        P("dp", "ctx", None, None, None),
        P("dp", "ctx", None, None, None),
        P("dp", "ctx", None, None, None),
        P("dp", "ctx", None, None, None),
        P(),
    )
    return jax.shard_map(
        per_device, mesh=mesh, in_specs=in_specs, out_specs=out_specs, check_vma=False
    )
```

```python
import math

import jax
import jax.numpy as jnp
from jax import lax
from jax.experimental import pallas as pl
from jax.experimental.pallas import tpu as pltpu
from jax.sharding import PartitionSpec as P

HEADS = 32
KV_HEADS = 4
HEAD_DIM = 128
GROUP = 8
REACH = 1


def shift_up(x, axis):
    size = lax.axis_size(axis)
    return lax.ppermute(x, axis, [(i, i + 1) for i in range(size - 1)])


def shift_down(x, axis):
    size = lax.axis_size(axis)
    return lax.ppermute(x, axis, [(i + 1, i) for i in range(size - 1)])


def swap_pairs(x, axis, offset):
    size = lax.axis_size(axis)
    pairs = []
    for i in range(size):
        partner = i + 1 if (i - offset) % 2 == 0 else i - 1
        if 0 <= partner < size:
            pairs.append((i, partner))
    return lax.ppermute(x, axis, pairs)


def neighbour_swap(to_next, to_prev, axis):
    even = lax.axis_index(axis) % 2 == 0
    first, second = lax.optimization_barrier(
        (jnp.where(even, to_next, to_prev), jnp.where(even, to_prev, to_next))
    )
    got_first = swap_pairs(first, axis, 0)
    got_second = swap_pairs(second, axis, 1)
    from_prev = jnp.where(even, got_second, got_first)
    from_next = jnp.where(even, got_first, got_second)
    return from_prev, from_next


def all_sum(x, axes):
    count = 1
    for axis in axes:
        count *= lax.axis_size(axis)
    spread = jnp.broadcast_to(x[None], (count,) + x.shape)
    return jnp.sum(lax.all_to_all(spread, axes, 0, 0, tiled=True), axis=0)


def group_kernel(
    sink_ref, q_ref, g_ref, k_ref, v_ref, allow_ref, o_ref, dq_ref, dk_ref, dv_ref, st_ref
):
    rows = q_ref.shape[1]
    score_scale = 1.0 / math.sqrt(HEAD_DIM)
    contract_last = (((1,), (1,)), ((), ()))
    contract_first = (((0,), (0,)), ((), ()))
    allowed = jnp.concatenate([allow_ref[0]] * GROUP, axis=0) > 0.5
    head_of_row = lax.broadcasted_iota(jnp.int32, (GROUP * rows, 1), 0) // rows
    for group in range(KV_HEADS):
        heads = [pl.ds((group * GROUP + h) * HEAD_DIM, HEAD_DIM) for h in range(GROUP)]
        side = pl.ds(group * HEAD_DIM, HEAD_DIM)
        query = jnp.concatenate([q_ref[0, :, cols] for cols in heads], axis=0)
        grad = jnp.concatenate([g_ref[0, :, cols] for cols in heads], axis=0)
        key = k_ref[0, :, side]
        value = v_ref[0, :, side]
        sink = jnp.zeros((GROUP * rows, 1), jnp.float32)
        for h in range(GROUP):
            sink = jnp.where(head_of_row == h, sink_ref[group * GROUP + h], sink)
        scores = (
            lax.dot_general(query, key, contract_last, preferred_element_type=jnp.float32)
            * score_scale
        )
        masked = jnp.where(allowed, scores, -jnp.inf)
        row_top = jnp.maximum(sink, jnp.max(masked, axis=1, keepdims=True))
        shifted = jnp.exp(masked - row_top)
        sink_weight = jnp.exp(sink - row_top)
        inverse_total = 1.0 / (sink_weight + jnp.sum(shifted, axis=1, keepdims=True))
        probs = shifted * inverse_total
        weights = probs.astype(jnp.bfloat16)
        attended = jnp.dot(weights, value, preferred_element_type=jnp.float32).astype(
            jnp.bfloat16
        )
        row_delta = jnp.sum(
            grad.astype(jnp.float32) * attended.astype(jnp.float32), axis=1, keepdims=True
        )
        dprob = lax.dot_general(grad, value, contract_last, preferred_element_type=jnp.float32)
        dscore = (probs * (dprob - row_delta)).astype(jnp.bfloat16)
        dquery = jnp.dot(dscore, key, preferred_element_type=jnp.float32) * score_scale
        dk_ref[0, :, side] = (
            lax.dot_general(dscore, query, contract_first, preferred_element_type=jnp.float32)
            * score_scale
        )
        dv_ref[0, :, side] = lax.dot_general(
            weights, grad, contract_first, preferred_element_type=jnp.float32
        )
        sink_share = sink_weight * inverse_total * row_delta
        for h in range(GROUP):
            part = slice(h * rows, (h + 1) * rows)
            o_ref[0, :, heads[h]] = attended[part]
            dq_ref[0, :, heads[h]] = dquery[part].astype(jnp.bfloat16)
            total = -jnp.sum(sink_share[part], axis=0, keepdims=True)
            st_ref[0, group, pl.ds(h, 1), :] = jnp.broadcast_to(total, (1, 128))


def attend_blocks(sink_logit, queries, out_grad, window, allowed):
    lanes, rows, query_width = queries.shape
    span = window.shape[1]
    side_width = KV_HEADS * HEAD_DIM
    row_spec = pl.BlockSpec((1, rows, query_width), lambda lane: (lane, 0, 0))
    side_spec = pl.BlockSpec((1, span, side_width), lambda lane: (lane, 0, 0))
    flops = 2 * lanes * HEADS * rows * span * HEAD_DIM * 6
    moved = 2 * (4 * queries.size + 2 * window.size) + 4 * allowed.size + 8 * window.size
    return pl.pallas_call(
        group_kernel,
        grid=(lanes,),
        in_specs=[
            pl.BlockSpec(memory_space=pltpu.SMEM),
            row_spec,
            row_spec,
            side_spec,
            pl.BlockSpec((1, span, side_width), lambda lane: (lane, 0, 1)),
            pl.BlockSpec((1, rows, span), lambda lane: (lane, 0, 0)),
        ],
        out_specs=[
            row_spec,
            row_spec,
            side_spec,
            side_spec,
            pl.BlockSpec((1, KV_HEADS, GROUP, 128), lambda lane: (lane, 0, 0, 0)),
        ],
        out_shape=[
            jax.ShapeDtypeStruct((lanes, rows, query_width), jnp.bfloat16),
            jax.ShapeDtypeStruct((lanes, rows, query_width), jnp.bfloat16),
            jax.ShapeDtypeStruct((lanes, span, side_width), jnp.float32),
            jax.ShapeDtypeStruct((lanes, span, side_width), jnp.float32),
            jax.ShapeDtypeStruct((lanes, KV_HEADS, GROUP, 128), jnp.float32),
        ],
        cost_estimate=pl.CostEstimate(
            flops=flops, transcendentals=2 * lanes * HEADS * rows * span, bytes_accessed=moved
        ),
    )(sink_logit, queries, out_grad, window, window, allowed)


def per_device(queries, keys, values, doc_bounds, sink_logit, out_grad):
    block_rows = queries.shape[3]
    query_width = queries.shape[4]
    value_width = keys.shape[4]
    pair_count = lax.axis_size("ctx")
    my_index = lax.axis_index("ctx")
    score_scale = 1.0 / math.sqrt(HEAD_DIM)
    at_fold = my_index == pair_count - 1
    last_block = 2 * pair_count - 1
    span = (REACH + 1) * block_rows

    own_pair = jnp.concatenate(
        [keys.reshape(2, block_rows, value_width), values.reshape(2, block_rows, value_width)], axis=2
    )
    prev0, prev1 = neighbour_swap(own_pair[0], own_pair[1], "ctx")
    prev1 = jnp.where(at_fold, own_pair[0], prev1)
    prev_pair = jnp.stack([prev0, prev1])
    window = jnp.concatenate([prev_pair, own_pair], axis=1)

    lane_block = jnp.stack([my_index, last_block - my_index]).astype(jnp.int32)
    row_offsets = jnp.arange(block_rows, dtype=jnp.int32)
    window_offsets = jnp.arange(span, dtype=jnp.int32)
    query_pos = lane_block[:, None] * block_rows + row_offsets[None, :]
    key_pos = (lane_block[:, None] - REACH) * block_rows + window_offsets[None, :]
    first_pos = doc_bounds.reshape(2, 2, block_rows)[:, 0]
    allowed = (key_pos[:, None, :] <= query_pos[:, :, None]) & (
        key_pos[:, None, :] >= first_pos[:, :, None]
    )
    attended, dquery, key_part, value_part, sink_parts = attend_blocks(
        sink_logit,
        queries.reshape(2, block_rows, query_width),
        out_grad.reshape(2, block_rows, query_width),
        window,
        allowed.astype(jnp.float32),
    )
    sink_terms = jnp.sum(sink_parts[:, :, :, 0], axis=0)
    sink_grad = all_sum(sink_terms.reshape(HEADS), ("ctx", "dp"))
    partial = jnp.concatenate([key_part, value_part], axis=2)

    prev_part = partial[:, :block_rows].astype(jnp.bfloat16)
    into1, into0 = neighbour_swap(prev_part[1], prev_part[0], "ctx")
    into0 = jnp.where(at_fold, prev_part[1], into0)
    own_part = partial[:, block_rows:]
    gathered = own_part + jnp.stack([into0, into1]).astype(jnp.float32)

    out_shape = (1, 1, 2, block_rows, query_width)
    pair_out = (1, 1, 2, block_rows, value_width)
    attn_out = attended.reshape(out_shape)
    query_grad = dquery.reshape(out_shape)
    key_grad = gathered[:, :, :value_width].astype(jnp.bfloat16).reshape(pair_out)
    value_grad = gathered[:, :, value_width:].astype(jnp.bfloat16).reshape(pair_out)
    return (attn_out, query_grad, key_grad, value_grad, sink_grad)


def solution(mesh):
    in_specs = (
        P("dp", "ctx", None, None, None),
        P("dp", "ctx", None, None, None),
        P("dp", "ctx", None, None, None),
        P("dp", "ctx", None, None, None),
        P(),
        P("dp", "ctx", None, None, None),
    )
    out_specs = (
        P("dp", "ctx", None, None, None),
        P("dp", "ctx", None, None, None),
        P("dp", "ctx", None, None, None),
        P("dp", "ctx", None, None, None),
        P(),
    )
    return jax.shard_map(
        per_device, mesh=mesh, in_specs=in_specs, out_specs=out_specs, check_vma=False
    )
```

```python
import math

import jax
import jax.numpy as jnp
from jax import lax
from jax.experimental import pallas as pl
from jax.experimental.pallas import tpu as pltpu
from jax.sharding import PartitionSpec as P

HEADS = 32
KV_HEADS = 4
HEAD_DIM = 128
GROUP = 8
REACH = 1


def shift_up(x, axis):
    size = lax.axis_size(axis)
    return lax.ppermute(x, axis, [(i, i + 1) for i in range(size - 1)])


def shift_down(x, axis):
    size = lax.axis_size(axis)
    return lax.ppermute(x, axis, [(i + 1, i) for i in range(size - 1)])


def swap_pairs(x, axis, offset):
    size = lax.axis_size(axis)
    pairs = []
    for i in range(size):
        partner = i + 1 if (i - offset) % 2 == 0 else i - 1
        if 0 <= partner < size:
            pairs.append((i, partner))
    return lax.ppermute(x, axis, pairs)


def neighbour_swap(to_next, to_prev, axis):
    even = lax.axis_index(axis) % 2 == 0
    first, second = lax.optimization_barrier(
        (jnp.where(even, to_next, to_prev), jnp.where(even, to_prev, to_next))
    )
    got_second = swap_pairs(second, axis, 1)
    got_first = swap_pairs(first, axis, 0)
    from_prev = jnp.where(even, got_second, got_first)
    from_next = jnp.where(even, got_first, got_second)
    return from_prev, from_next


def all_sum(x, axes):
    count = 1
    for axis in axes:
        count *= lax.axis_size(axis)
    spread = jnp.broadcast_to(x[None], (count,) + x.shape)
    return jnp.sum(lax.all_to_all(spread, axes, 0, 0, tiled=True), axis=0)


def group_kernel(
    sink_ref, q_ref, g_ref, k_ref, v_ref, allow_ref, o_ref, dq_ref, dk_ref, dv_ref, st_ref
):
    rows = q_ref.shape[1]
    score_scale = 1.0 / math.sqrt(HEAD_DIM)
    contract_last = (((1,), (1,)), ((), ()))
    contract_first = (((0,), (0,)), ((), ()))
    allowed = jnp.concatenate([allow_ref[0]] * GROUP, axis=0) > 0.5
    head_of_row = lax.broadcasted_iota(jnp.int32, (GROUP * rows, 1), 0) // rows
    for group in range(KV_HEADS):
        heads = [pl.ds((group * GROUP + h) * HEAD_DIM, HEAD_DIM) for h in range(GROUP)]
        side = pl.ds(group * HEAD_DIM, HEAD_DIM)
        query = jnp.concatenate([q_ref[0, :, cols] for cols in heads], axis=0)
        grad = jnp.concatenate([g_ref[0, :, cols] for cols in heads], axis=0)
        key = k_ref[0, :, side]
        value = v_ref[0, :, side]
        sink = jnp.zeros((GROUP * rows, 1), jnp.float32)
        for h in range(GROUP):
            sink = jnp.where(head_of_row == h, sink_ref[group * GROUP + h], sink)
        scores = (
            lax.dot_general(query, key, contract_last, preferred_element_type=jnp.float32)
            * score_scale
        )
        masked = jnp.where(allowed, scores, -jnp.inf)
        row_top = jnp.maximum(sink, jnp.max(masked, axis=1, keepdims=True))
        shifted = jnp.exp(masked - row_top)
        sink_weight = jnp.exp(sink - row_top)
        inverse_total = 1.0 / (sink_weight + jnp.sum(shifted, axis=1, keepdims=True))
        probs = shifted * inverse_total
        weights = probs.astype(jnp.bfloat16)
        attended = jnp.dot(weights, value, preferred_element_type=jnp.float32).astype(
            jnp.bfloat16
        )
        row_delta = jnp.sum(
            grad.astype(jnp.float32) * attended.astype(jnp.float32), axis=1, keepdims=True
        )
        dprob = lax.dot_general(grad, value, contract_last, preferred_element_type=jnp.float32)
        dscore = (probs * (dprob - row_delta)).astype(jnp.bfloat16)
        dquery = jnp.dot(dscore, key, preferred_element_type=jnp.float32) * score_scale
        dk_ref[0, :, side] = (
            lax.dot_general(dscore, query, contract_first, preferred_element_type=jnp.float32)
            * score_scale
        )
        dv_ref[0, :, side] = lax.dot_general(
            weights, grad, contract_first, preferred_element_type=jnp.float32
        )
        sink_share = sink_weight * inverse_total * row_delta
        for h in range(GROUP):
            part = slice(h * rows, (h + 1) * rows)
            o_ref[0, :, heads[h]] = attended[part]
            dq_ref[0, :, heads[h]] = dquery[part].astype(jnp.bfloat16)
            total = -jnp.sum(sink_share[part], axis=0, keepdims=True)
            st_ref[0, group, pl.ds(h, 1), :] = jnp.broadcast_to(total, (1, 128))


def attend_blocks(sink_logit, queries, out_grad, window, allowed):
    lanes, rows, query_width = queries.shape
    span = window.shape[1]
    side_width = KV_HEADS * HEAD_DIM
    row_spec = pl.BlockSpec((1, rows, query_width), lambda lane: (lane, 0, 0))
    side_spec = pl.BlockSpec((1, span, side_width), lambda lane: (lane, 0, 0))
    flops = 2 * lanes * HEADS * rows * span * HEAD_DIM * 6
    moved = 2 * (4 * queries.size + 2 * window.size) + 4 * allowed.size + 8 * window.size
    return pl.pallas_call(
        group_kernel,
        grid=(lanes,),
        in_specs=[
            pl.BlockSpec(memory_space=pltpu.SMEM),
            row_spec,
            row_spec,
            side_spec,
            pl.BlockSpec((1, span, side_width), lambda lane: (lane, 0, 1)),
            pl.BlockSpec((1, rows, span), lambda lane: (lane, 0, 0)),
        ],
        out_specs=[
            row_spec,
            row_spec,
            side_spec,
            side_spec,
            pl.BlockSpec((1, KV_HEADS, GROUP, 128), lambda lane: (lane, 0, 0, 0)),
        ],
        out_shape=[
            jax.ShapeDtypeStruct((lanes, rows, query_width), jnp.bfloat16),
            jax.ShapeDtypeStruct((lanes, rows, query_width), jnp.bfloat16),
            jax.ShapeDtypeStruct((lanes, span, side_width), jnp.float32),
            jax.ShapeDtypeStruct((lanes, span, side_width), jnp.float32),
            jax.ShapeDtypeStruct((lanes, KV_HEADS, GROUP, 128), jnp.float32),
        ],
        cost_estimate=pl.CostEstimate(
            flops=flops, transcendentals=2 * lanes * HEADS * rows * span, bytes_accessed=moved
        ),
    )(sink_logit, queries, out_grad, window, window, allowed)


def per_device(queries, keys, values, doc_bounds, sink_logit, out_grad):
    block_rows = queries.shape[3]
    query_width = queries.shape[4]
    value_width = keys.shape[4]
    pair_count = lax.axis_size("ctx")
    my_index = lax.axis_index("ctx")
    score_scale = 1.0 / math.sqrt(HEAD_DIM)
    at_fold = my_index == pair_count - 1
    last_block = 2 * pair_count - 1
    span = (REACH + 1) * block_rows

    own_pair = jnp.concatenate(
        [keys.reshape(2, block_rows, value_width), values.reshape(2, block_rows, value_width)], axis=2
    )
    prev0, prev1 = neighbour_swap(own_pair[0], own_pair[1], "ctx")
    prev1 = jnp.where(at_fold, own_pair[0], prev1)
    prev_pair = jnp.stack([prev0, prev1])
    window = jnp.concatenate([prev_pair, own_pair], axis=1)

    lane_block = jnp.stack([my_index, last_block - my_index]).astype(jnp.int32)
    row_offsets = jnp.arange(block_rows, dtype=jnp.int32)
    window_offsets = jnp.arange(span, dtype=jnp.int32)
    query_pos = lane_block[:, None] * block_rows + row_offsets[None, :]
    key_pos = (lane_block[:, None] - REACH) * block_rows + window_offsets[None, :]
    first_pos = doc_bounds.reshape(2, 2, block_rows)[:, 0]
    allowed = (key_pos[:, None, :] <= query_pos[:, :, None]) & (
        key_pos[:, None, :] >= first_pos[:, :, None]
    )
    attended, dquery, key_part, value_part, sink_parts = attend_blocks(
        sink_logit,
        queries.reshape(2, block_rows, query_width),
        out_grad.reshape(2, block_rows, query_width),
        window,
        allowed.astype(jnp.float32),
    )
    sink_terms = jnp.sum(sink_parts[:, :, :, 0], axis=0)
    sink_grad = all_sum(sink_terms.reshape(HEADS), ("ctx", "dp"))
    partial = jnp.concatenate([key_part, value_part], axis=2)

    prev_part = partial[:, :block_rows].astype(jnp.bfloat16)
    into1, into0 = neighbour_swap(prev_part[1], prev_part[0], "ctx")
    into0 = jnp.where(at_fold, prev_part[1], into0)
    own_part = partial[:, block_rows:]
    gathered = own_part + jnp.stack([into0, into1]).astype(jnp.float32)

    out_shape = (1, 1, 2, block_rows, query_width)
    pair_out = (1, 1, 2, block_rows, value_width)
    attn_out = attended.reshape(out_shape)
    query_grad = dquery.reshape(out_shape)
    key_grad = gathered[:, :, :value_width].astype(jnp.bfloat16).reshape(pair_out)
    value_grad = gathered[:, :, value_width:].astype(jnp.bfloat16).reshape(pair_out)
    return (attn_out, query_grad, key_grad, value_grad, sink_grad)


def solution(mesh):
    in_specs = (
        P("dp", "ctx", None, None, None),
        P("dp", "ctx", None, None, None),
        P("dp", "ctx", None, None, None),
        P("dp", "ctx", None, None, None),
        P(),
        P("dp", "ctx", None, None, None),
    )
    out_specs = (
        P("dp", "ctx", None, None, None),
        P("dp", "ctx", None, None, None),
        P("dp", "ctx", None, None, None),
        P("dp", "ctx", None, None, None),
        P(),
    )
    return jax.shard_map(
        per_device, mesh=mesh, in_specs=in_specs, out_specs=out_specs, check_vma=False
    )
```

```python
import math

import jax
import jax.numpy as jnp
from jax import lax
from jax.experimental import pallas as pl
from jax.experimental.pallas import tpu as pltpu
from jax.sharding import PartitionSpec as P

HEADS = 32
KV_HEADS = 4
HEAD_DIM = 128
GROUP = 8
REACH = 1


def shift_up(x, axis):
    size = lax.axis_size(axis)
    return lax.ppermute(x, axis, [(i, i + 1) for i in range(size - 1)])


def shift_down(x, axis):
    size = lax.axis_size(axis)
    return lax.ppermute(x, axis, [(i + 1, i) for i in range(size - 1)])


def swap_pairs(x, axis, offset):
    size = lax.axis_size(axis)
    pairs = []
    for i in range(size):
        partner = i + 1 if (i - offset) % 2 == 0 else i - 1
        if partner == size:
            partner = i
        if partner >= 0:
            pairs.append((i, partner))
    return lax.ppermute(x, axis, pairs)


def all_sum(x, axes):
    count = 1
    for axis in axes:
        count *= lax.axis_size(axis)
    spread = jnp.broadcast_to(x[None], (count,) + x.shape)
    return jnp.sum(lax.all_to_all(spread, axes, 0, 0, tiled=True), axis=0)


def group_kernel(lane_ref, sink_ref, q_ref, g_ref, k_ref, v_ref, prev_ref, allow_ref, *refs):
    o_ref, dq_ref, msg_ref, dk_ref, dv_ref, st_ref = refs[-6:]
    rows = q_ref.shape[1]
    score_scale = 1.0 / math.sqrt(HEAD_DIM)
    contract_last = (((1,), (1,)), ((), ()))
    contract_first = (((0,), (0,)), ((), ()))
    allowed = jnp.concatenate([allow_ref[0]] * GROUP, axis=0) > 0.5
    head_of_row = lax.broadcasted_iota(jnp.int32, (GROUP * rows, 1), 0) // rows
    for group in range(KV_HEADS):
        heads = [pl.ds((group * GROUP + h) * HEAD_DIM, HEAD_DIM) for h in range(GROUP)]
        side = pl.ds(group * HEAD_DIM, HEAD_DIM)
        query = jnp.concatenate([q_ref[0, :, cols] for cols in heads], axis=0)
        grad = jnp.concatenate([g_ref[0, :, cols] for cols in heads], axis=0)
        value_side = pl.ds((KV_HEADS + group) * HEAD_DIM, HEAD_DIM)
        key = jnp.concatenate([prev_ref[:, side], k_ref[0, :, side]], axis=0)
        value = jnp.concatenate([prev_ref[:, value_side], v_ref[0, :, side]], axis=0)
        sink = jnp.zeros((GROUP * rows, 1), jnp.float32)
        for h in range(GROUP):
            sink = jnp.where(head_of_row == h, sink_ref[group * GROUP + h], sink)
        scores = (
            lax.dot_general(query, key, contract_last, preferred_element_type=jnp.float32)
            * score_scale
        )
        masked = jnp.where(allowed, scores, -jnp.inf)
        row_top = jnp.maximum(sink, jnp.max(masked, axis=1, keepdims=True))
        shifted = jnp.exp(masked - row_top)
        sink_weight = jnp.exp(sink - row_top)
        inverse_total = 1.0 / (sink_weight + jnp.sum(shifted, axis=1, keepdims=True))
        probs = shifted * inverse_total
        weights = probs.astype(jnp.bfloat16)
        attended = jnp.dot(weights, value, preferred_element_type=jnp.float32).astype(
            jnp.bfloat16
        )
        row_delta = jnp.sum(
            grad.astype(jnp.float32) * attended.astype(jnp.float32), axis=1, keepdims=True
        )
        dprob = lax.dot_general(grad, value, contract_last, preferred_element_type=jnp.float32)
        dscore = (probs * (dprob - row_delta)).astype(jnp.bfloat16)
        dquery = jnp.dot(dscore, key, preferred_element_type=jnp.float32) * score_scale
        dkey = (
            lax.dot_general(dscore, query, contract_first, preferred_element_type=jnp.float32)
            * score_scale
        )
        dvalue = lax.dot_general(weights, grad, contract_first, preferred_element_type=jnp.float32)
        msg_ref[:, side] = dkey[:rows].astype(jnp.bfloat16)
        msg_ref[:, value_side] = dvalue[:rows].astype(jnp.bfloat16)
        dk_ref[0, :, side] = dkey[rows:]
        dv_ref[0, :, side] = dvalue[rows:]
        sink_share = sink_weight * inverse_total * row_delta
        for h in range(GROUP):
            part = slice(h * rows, (h + 1) * rows)
            o_ref[0, :, heads[h]] = attended[part]
            dq_ref[0, :, heads[h]] = dquery[part].astype(jnp.bfloat16)
            total = -jnp.sum(sink_share[part], axis=0, keepdims=True)
            st_ref[group, pl.ds(h, 1), :] = jnp.broadcast_to(total, (1, 128))


def attend_lane(lane, sink_logit, queries, out_grad, keys, values, prev, allowed, earlier=None):
    lanes, rows, query_width = queries.shape
    side_width = keys.shape[2]
    pair_width = prev.shape[1]
    lane_block = lambda width: pl.BlockSpec((1, rows, width), lambda i, lane_ref: (lane_ref[0], 0, 0))
    flops = 2 * HEADS * rows * 2 * rows * HEAD_DIM * 6
    moved = 4 * queries.size + 3 * keys.size + 8 * prev.size + 2 * allowed.size
    in_specs = [
        pl.BlockSpec(memory_space=pltpu.SMEM),
        lane_block(query_width),
        lane_block(query_width),
        lane_block(side_width),
        lane_block(side_width),
        pl.BlockSpec((rows, pair_width), lambda i, lane_ref: (0, 0)),
        pl.BlockSpec((1, rows, 2 * rows), lambda i, lane_ref: (lane_ref[0], 0, 0)),
    ]
    operands = [lane, sink_logit, queries, out_grad, keys, values, prev, allowed]
    aliases = {}
    if earlier is not None:
        for out_index, array in zip((0, 1, 3, 4), earlier):
            aliases[len(operands)] = out_index
            in_specs.append(pl.BlockSpec(memory_space=pl.ANY))
            operands.append(array)
    grid_spec = pltpu.PrefetchScalarGridSpec(
        num_scalar_prefetch=1,
        grid=(1,),
        in_specs=in_specs,
        out_specs=[
            lane_block(query_width),
            lane_block(query_width),
            pl.BlockSpec((rows, pair_width), lambda i, lane_ref: (0, 0)),
            lane_block(side_width),
            lane_block(side_width),
            pl.BlockSpec((KV_HEADS, GROUP, 128), lambda i, lane_ref: (0, 0, 0)),
        ],
    )
    return pl.pallas_call(
        group_kernel,
        grid_spec=grid_spec,
        out_shape=[
            jax.ShapeDtypeStruct((lanes, rows, query_width), jnp.bfloat16),
            jax.ShapeDtypeStruct((lanes, rows, query_width), jnp.bfloat16),
            jax.ShapeDtypeStruct((rows, pair_width), jnp.bfloat16),
            jax.ShapeDtypeStruct((lanes, rows, side_width), jnp.float32),
            jax.ShapeDtypeStruct((lanes, rows, side_width), jnp.float32),
            jax.ShapeDtypeStruct((KV_HEADS, GROUP, 128), jnp.float32),
        ],
        input_output_aliases=aliases,
        cost_estimate=pl.CostEstimate(
            flops=flops, transcendentals=2 * HEADS * rows * 2 * rows, bytes_accessed=moved
        ),
    )(*operands)


def per_device(queries, keys, values, doc_bounds, sink_logit, out_grad):
    block_rows = queries.shape[3]
    query_width = queries.shape[4]
    value_width = keys.shape[4]
    pair_count = lax.axis_size("ctx")
    my_index = lax.axis_index("ctx")
    score_scale = 1.0 / math.sqrt(HEAD_DIM)
    last_block = 2 * pair_count - 1
    span = (REACH + 1) * block_rows

    key_lanes = keys.reshape(2, block_rows, value_width)
    value_lanes = values.reshape(2, block_rows, value_width)
    even = (my_index % 2 == 0).astype(jnp.int32)

    def lane_pair(lane):
        return jnp.concatenate(
            [
                lax.dynamic_index_in_dim(key_lanes, lane, keepdims=False),
                lax.dynamic_index_in_dim(value_lanes, lane, keepdims=False),
            ],
            axis=1,
        )

    near_send, far_send = lax.optimization_barrier((lane_pair(1 - even), lane_pair(even)))
    far_prev = swap_pairs(far_send, "ctx", 1)
    near_prev = swap_pairs(near_send, "ctx", 0)

    lane_block = jnp.stack([my_index, last_block - my_index]).astype(jnp.int32)
    row_offsets = jnp.arange(block_rows, dtype=jnp.int32)
    window_offsets = jnp.arange(span, dtype=jnp.int32)
    query_pos = lane_block[:, None] * block_rows + row_offsets[None, :]
    key_pos = (lane_block[:, None] - REACH) * block_rows + window_offsets[None, :]
    first_pos = doc_bounds.reshape(2, 2, block_rows)[:, 0]
    allowed = (key_pos[:, None, :] <= query_pos[:, :, None]) & (
        key_pos[:, None, :] >= first_pos[:, :, None]
    )
    common = (
        sink_logit,
        queries.reshape(2, block_rows, query_width),
        out_grad.reshape(2, block_rows, query_width),
        key_lanes,
        value_lanes,
    )
    mask = allowed.astype(jnp.float32)
    near = attend_lane(even.reshape(1), *common, near_prev, mask)
    got_far = swap_pairs(near[2], "ctx", 0)
    far = attend_lane(
        (1 - even).reshape(1), *common, far_prev, mask, (near[0], near[1], near[3], near[4])
    )
    attended, dquery, _, key_own, value_own, _ = far
    sink_terms = (near[5] + far[5])[:, :, 0]
    sink_grad = all_sum(sink_terms.reshape(HEADS), ("ctx", "dp"))
    got_near = swap_pairs(far[2], "ctx", 1)
    is_even = even == 1
    arrived = jnp.stack(
        [jnp.where(is_even, got_far, got_near), jnp.where(is_even, got_near, got_far)]
    ).astype(jnp.float32)

    out_shape = (1, 1, 2, block_rows, query_width)
    pair_out = (1, 1, 2, block_rows, value_width)
    attn_out = attended.reshape(out_shape)
    query_grad = dquery.reshape(out_shape)
    key_grad = (key_own + arrived[:, :, :value_width]).astype(jnp.bfloat16).reshape(pair_out)
    value_grad = (value_own + arrived[:, :, value_width:]).astype(jnp.bfloat16).reshape(pair_out)
    return (attn_out, query_grad, key_grad, value_grad, sink_grad)


def solution(mesh):
    in_specs = (
        P("dp", "ctx", None, None, None),
        P("dp", "ctx", None, None, None),
        P("dp", "ctx", None, None, None),
        P("dp", "ctx", None, None, None),
        P(),
        P("dp", "ctx", None, None, None),
    )
    out_specs = (
        P("dp", "ctx", None, None, None),
        P("dp", "ctx", None, None, None),
        P("dp", "ctx", None, None, None),
        P("dp", "ctx", None, None, None),
        P(),
    )
    return jax.shard_map(
        per_device, mesh=mesh, in_specs=in_specs, out_specs=out_specs, check_vma=False
    )
```

```python
import math

import jax
import jax.numpy as jnp
from jax import lax
from jax.experimental import pallas as pl
from jax.experimental.pallas import tpu as pltpu
from jax.sharding import PartitionSpec as P

HEADS = 32
KV_HEADS = 4
HEAD_DIM = 128
GROUP = 8
REACH = 1


def shift_up(x, axis):
    size = lax.axis_size(axis)
    return lax.ppermute(x, axis, [(i, i + 1) for i in range(size - 1)])


def shift_down(x, axis):
    size = lax.axis_size(axis)
    return lax.ppermute(x, axis, [(i + 1, i) for i in range(size - 1)])


def swap_pairs(x, axis, offset):
    size = lax.axis_size(axis)
    pairs = []
    for i in range(size):
        partner = i + 1 if (i - offset) % 2 == 0 else i - 1
        if 0 <= partner < size:
            pairs.append((i, partner))
    return lax.ppermute(x, axis, pairs)


def neighbour_swap(to_next, to_prev, axis):
    even = lax.axis_index(axis) % 2 == 0
    first, second = lax.optimization_barrier(
        (jnp.where(even, to_next, to_prev), jnp.where(even, to_prev, to_next))
    )
    got_first = swap_pairs(first, axis, 0)
    got_second = swap_pairs(second, axis, 1)
    from_prev = jnp.where(even, got_second, got_first)
    from_next = jnp.where(even, got_first, got_second)
    return from_prev, from_next


def all_sum(x, axes):
    count = 1
    for axis in axes:
        count *= lax.axis_size(axis)
    spread = jnp.broadcast_to(x[None], (count,) + x.shape)
    return jnp.sum(lax.all_to_all(spread, axes, 0, 0, tiled=True), axis=0)


def group_kernel(
    sink_ref, q_ref, g_ref, k_ref, v_ref, allow_ref, o_ref, dq_ref, dk_ref, dv_ref, st_ref
):
    rows = q_ref.shape[1]
    score_scale = 1.0 / math.sqrt(HEAD_DIM)
    contract_last = (((1,), (1,)), ((), ()))
    contract_first = (((0,), (0,)), ((), ()))
    allowed = jnp.concatenate([allow_ref[0]] * GROUP, axis=0) > 0.5
    head_of_row = lax.broadcasted_iota(jnp.int32, (GROUP * rows, 1), 0) // rows
    groups = k_ref.shape[2] // HEAD_DIM
    for group in range(groups):
        first_head = (pl.program_id(1) * groups + group) * GROUP
        heads = [pl.ds((group * GROUP + h) * HEAD_DIM, HEAD_DIM) for h in range(GROUP)]
        side = pl.ds(group * HEAD_DIM, HEAD_DIM)
        query = jnp.concatenate([q_ref[0, :, cols] for cols in heads], axis=0)
        grad = jnp.concatenate([g_ref[0, :, cols] for cols in heads], axis=0)
        key = k_ref[0, :, side]
        value = v_ref[0, :, side]
        sink = jnp.zeros((GROUP * rows, 1), jnp.float32)
        for h in range(GROUP):
            sink = jnp.where(head_of_row == h, sink_ref[first_head + h], sink)
        scores = (
            lax.dot_general(query, key, contract_last, preferred_element_type=jnp.float32)
            * score_scale
        )
        masked = jnp.where(allowed, scores, -jnp.inf)
        row_top = jnp.maximum(sink, jnp.max(masked, axis=1, keepdims=True))
        shifted = jnp.exp(masked - row_top)
        sink_weight = jnp.exp(sink - row_top)
        inverse_total = 1.0 / (sink_weight + jnp.sum(shifted, axis=1, keepdims=True))
        probs = shifted * inverse_total
        weights = probs.astype(jnp.bfloat16)
        attended = jnp.dot(weights, value, preferred_element_type=jnp.float32).astype(
            jnp.bfloat16
        )
        row_delta = jnp.sum(
            grad.astype(jnp.float32) * attended.astype(jnp.float32), axis=1, keepdims=True
        )
        dprob = lax.dot_general(grad, value, contract_last, preferred_element_type=jnp.float32)
        dscore = (probs * (dprob - row_delta)).astype(jnp.bfloat16)
        dquery = jnp.dot(dscore, key, preferred_element_type=jnp.float32) * score_scale
        dk_ref[0, :, side] = (
            lax.dot_general(dscore, query, contract_first, preferred_element_type=jnp.float32)
            * score_scale
        )
        dv_ref[0, :, side] = lax.dot_general(
            weights, grad, contract_first, preferred_element_type=jnp.float32
        )
        sink_share = sink_weight * inverse_total * row_delta
        for h in range(GROUP):
            part = slice(h * rows, (h + 1) * rows)
            o_ref[0, :, heads[h]] = attended[part]
            dq_ref[0, :, heads[h]] = dquery[part].astype(jnp.bfloat16)
            total = -jnp.sum(sink_share[part], axis=0, keepdims=True)
            st_ref[0, group, pl.ds(h, 1), :] = jnp.broadcast_to(total, (1, 128))


def attend_blocks(sink_logit, queries, out_grad, window, allowed):
    lanes, rows, query_width = queries.shape
    span = window.shape[1]
    halves = 2
    groups = KV_HEADS // halves
    lane_half = lambda lane, half: (lane, 0, half)
    row_spec = pl.BlockSpec((1, rows, groups * GROUP * HEAD_DIM), lane_half)
    side_spec = pl.BlockSpec((1, span, groups * HEAD_DIM), lane_half)
    flops = 2 * lanes * HEADS * rows * span * HEAD_DIM * 6
    moved = 2 * (4 * queries.size + 2 * window.size) + 4 * allowed.size + 8 * window.size
    return pl.pallas_call(
        group_kernel,
        grid=(lanes, halves),
        in_specs=[
            pl.BlockSpec(memory_space=pltpu.SMEM),
            row_spec,
            row_spec,
            side_spec,
            pl.BlockSpec((1, span, groups * HEAD_DIM), lambda lane, half: (lane, 0, halves + half)),
            pl.BlockSpec((1, rows, span), lambda lane, half: (lane, 0, 0)),
        ],
        out_specs=[
            row_spec,
            row_spec,
            side_spec,
            side_spec,
            pl.BlockSpec((1, groups, GROUP, 128), lambda lane, half: (lane, half, 0, 0)),
        ],
        out_shape=[
            jax.ShapeDtypeStruct((lanes, rows, query_width), jnp.bfloat16),
            jax.ShapeDtypeStruct((lanes, rows, query_width), jnp.bfloat16),
            jax.ShapeDtypeStruct((lanes, span, KV_HEADS * HEAD_DIM), jnp.float32),
            jax.ShapeDtypeStruct((lanes, span, KV_HEADS * HEAD_DIM), jnp.float32),
            jax.ShapeDtypeStruct((lanes, KV_HEADS, GROUP, 128), jnp.float32),
        ],
        cost_estimate=pl.CostEstimate(
            flops=flops, transcendentals=2 * lanes * HEADS * rows * span, bytes_accessed=moved
        ),
    )(sink_logit, queries, out_grad, window, window, allowed)


def per_device(queries, keys, values, doc_bounds, sink_logit, out_grad):
    block_rows = queries.shape[3]
    query_width = queries.shape[4]
    value_width = keys.shape[4]
    pair_count = lax.axis_size("ctx")
    my_index = lax.axis_index("ctx")
    score_scale = 1.0 / math.sqrt(HEAD_DIM)
    at_fold = my_index == pair_count - 1
    last_block = 2 * pair_count - 1
    span = (REACH + 1) * block_rows

    own_pair = jnp.concatenate(
        [keys.reshape(2, block_rows, value_width), values.reshape(2, block_rows, value_width)], axis=2
    )
    prev0, prev1 = neighbour_swap(own_pair[0], own_pair[1], "ctx")
    prev1 = jnp.where(at_fold, own_pair[0], prev1)
    prev_pair = jnp.stack([prev0, prev1])
    window = jnp.concatenate([prev_pair, own_pair], axis=1)

    lane_block = jnp.stack([my_index, last_block - my_index]).astype(jnp.int32)
    row_offsets = jnp.arange(block_rows, dtype=jnp.int32)
    window_offsets = jnp.arange(span, dtype=jnp.int32)
    query_pos = lane_block[:, None] * block_rows + row_offsets[None, :]
    key_pos = (lane_block[:, None] - REACH) * block_rows + window_offsets[None, :]
    first_pos = doc_bounds.reshape(2, 2, block_rows)[:, 0]
    allowed = (key_pos[:, None, :] <= query_pos[:, :, None]) & (
        key_pos[:, None, :] >= first_pos[:, :, None]
    )
    attended, dquery, key_part, value_part, sink_parts = attend_blocks(
        sink_logit,
        queries.reshape(2, block_rows, query_width),
        out_grad.reshape(2, block_rows, query_width),
        window,
        allowed.astype(jnp.float32),
    )
    sink_terms = jnp.sum(sink_parts[:, :, :, 0], axis=0)
    sink_grad = all_sum(sink_terms.reshape(HEADS), ("ctx", "dp"))
    partial = jnp.concatenate([key_part, value_part], axis=2)

    prev_part = partial[:, :block_rows].astype(jnp.bfloat16)
    into1, into0 = neighbour_swap(prev_part[1], prev_part[0], "ctx")
    into0 = jnp.where(at_fold, prev_part[1], into0)
    own_part = partial[:, block_rows:]
    gathered = own_part + jnp.stack([into0, into1]).astype(jnp.float32)

    out_shape = (1, 1, 2, block_rows, query_width)
    pair_out = (1, 1, 2, block_rows, value_width)
    attn_out = attended.reshape(out_shape)
    query_grad = dquery.reshape(out_shape)
    key_grad = gathered[:, :, :value_width].astype(jnp.bfloat16).reshape(pair_out)
    value_grad = gathered[:, :, value_width:].astype(jnp.bfloat16).reshape(pair_out)
    return (attn_out, query_grad, key_grad, value_grad, sink_grad)


def solution(mesh):
    in_specs = (
        P("dp", "ctx", None, None, None),
        P("dp", "ctx", None, None, None),
        P("dp", "ctx", None, None, None),
        P("dp", "ctx", None, None, None),
        P(),
        P("dp", "ctx", None, None, None),
    )
    out_specs = (
        P("dp", "ctx", None, None, None),
        P("dp", "ctx", None, None, None),
        P("dp", "ctx", None, None, None),
        P("dp", "ctx", None, None, None),
        P(),
    )
    return jax.shard_map(
        per_device, mesh=mesh, in_specs=in_specs, out_specs=out_specs, check_vma=False
    )
```

```python
import math

import jax
import jax.numpy as jnp
from jax import lax
from jax.experimental import pallas as pl
from jax.experimental.pallas import tpu as pltpu
from jax.sharding import PartitionSpec as P

HEADS = 32
KV_HEADS = 4
HEAD_DIM = 128
GROUP = 8
REACH = 1


def shift_up(x, axis):
    size = lax.axis_size(axis)
    return lax.ppermute(x, axis, [(i, i + 1) for i in range(size - 1)])


def shift_down(x, axis):
    size = lax.axis_size(axis)
    return lax.ppermute(x, axis, [(i + 1, i) for i in range(size - 1)])


def swap_pairs(x, axis, offset):
    size = lax.axis_size(axis)
    pairs = []
    for i in range(size):
        partner = i + 1 if (i - offset) % 2 == 0 else i - 1
        if 0 <= partner < size:
            pairs.append((i, partner))
    return lax.ppermute(x, axis, pairs)


def neighbour_swap(to_next, to_prev, axis):
    even = lax.axis_index(axis) % 2 == 0
    first, second = lax.optimization_barrier(
        (jnp.where(even, to_next, to_prev), jnp.where(even, to_prev, to_next))
    )
    got_first = swap_pairs(first, axis, 0)
    got_second = swap_pairs(second, axis, 1)
    from_prev = jnp.where(even, got_second, got_first)
    from_next = jnp.where(even, got_first, got_second)
    return from_prev, from_next


def all_sum(x, axes):
    count = 1
    for axis in axes:
        count *= lax.axis_size(axis)
    spread = jnp.broadcast_to(x[None], (count,) + x.shape)
    return jnp.sum(lax.all_to_all(spread, axes, 0, 0, tiled=True), axis=0)


def group_kernel(
    flag_ref, sink_ref, q_ref, g_ref, k_ref, v_ref, allow_ref,
    o_ref, dq_ref, msg_ref, dk_ref, dv_ref, st_ref,
):
    rows = q_ref.shape[1]
    score_scale = 1.0 / math.sqrt(HEAD_DIM)
    contract_last = (((1,), (1,)), ((), ()))
    contract_first = (((0,), (0,)), ((), ()))
    allowed = jnp.concatenate([allow_ref[0]] * GROUP, axis=0) > 0.5
    head_of_row = lax.broadcasted_iota(jnp.int32, (GROUP * rows, 1), 0) // rows
    for group in range(KV_HEADS):
        heads = [pl.ds((group * GROUP + h) * HEAD_DIM, HEAD_DIM) for h in range(GROUP)]
        side = pl.ds(group * HEAD_DIM, HEAD_DIM)
        query = jnp.concatenate([q_ref[0, :, cols] for cols in heads], axis=0)
        grad = jnp.concatenate([g_ref[0, :, cols] for cols in heads], axis=0)
        key = k_ref[0, :, side]
        value = v_ref[0, :, side]
        sink = jnp.zeros((GROUP * rows, 1), jnp.float32)
        for h in range(GROUP):
            sink = jnp.where(head_of_row == h, sink_ref[group * GROUP + h], sink)
        scores = (
            lax.dot_general(query, key, contract_last, preferred_element_type=jnp.float32)
            * score_scale
        )
        masked = jnp.where(allowed, scores, -jnp.inf)
        row_top = jnp.maximum(sink, jnp.max(masked, axis=1, keepdims=True))
        shifted = jnp.exp(masked - row_top)
        sink_weight = jnp.exp(sink - row_top)
        inverse_total = 1.0 / (sink_weight + jnp.sum(shifted, axis=1, keepdims=True))
        probs = shifted * inverse_total
        weights = probs.astype(jnp.bfloat16)
        attended = jnp.dot(weights, value, preferred_element_type=jnp.float32).astype(
            jnp.bfloat16
        )
        row_delta = jnp.sum(
            grad.astype(jnp.float32) * attended.astype(jnp.float32), axis=1, keepdims=True
        )
        dprob = lax.dot_general(grad, value, contract_last, preferred_element_type=jnp.float32)
        dscore = (probs * (dprob - row_delta)).astype(jnp.bfloat16)
        dquery = jnp.dot(dscore, key, preferred_element_type=jnp.float32) * score_scale
        dkey = (
            lax.dot_general(dscore, query, contract_first, preferred_element_type=jnp.float32)
            * score_scale
        )
        dvalue = lax.dot_general(weights, grad, contract_first, preferred_element_type=jnp.float32)
        msg_ref[0, :, side] = dkey[:rows].astype(jnp.bfloat16)
        msg_ref[0, :, pl.ds((KV_HEADS + group) * HEAD_DIM, HEAD_DIM)] = dvalue[:rows].astype(
            jnp.bfloat16
        )
        dk_ref[0, :, side] = dkey[rows:]
        dv_ref[0, :, side] = dvalue[rows:]
        sink_share = sink_weight * inverse_total * row_delta
        for h in range(GROUP):
            part = slice(h * rows, (h + 1) * rows)
            o_ref[0, :, heads[h]] = attended[part]
            dq_ref[0, :, heads[h]] = dquery[part].astype(jnp.bfloat16)
            total = -jnp.sum(sink_share[part], axis=0, keepdims=True)
            st_ref[0, group, pl.ds(h, 1), :] = jnp.broadcast_to(total, (1, 128))


def attend_blocks(flag, sink_logit, queries, out_grad, window, allowed):
    lanes, rows, query_width = queries.shape
    span = window.shape[1]
    side_width = KV_HEADS * HEAD_DIM
    row_spec = pl.BlockSpec((1, rows, query_width), lambda lane, flag_ref: (lane, 0, 0))
    side_spec = pl.BlockSpec((1, span, side_width), lambda lane, flag_ref: (lane, 0, 0))
    own_spec = pl.BlockSpec((1, rows, side_width), lambda lane, flag_ref: (lane, 0, 0))
    flops = 2 * lanes * HEADS * rows * span * HEAD_DIM * 6
    moved = 2 * (4 * queries.size + 2 * window.size) + 4 * allowed.size + 6 * window.size
    grid_spec = pltpu.PrefetchScalarGridSpec(
        num_scalar_prefetch=1,
        grid=(lanes,),
        in_specs=[
            pl.BlockSpec(memory_space=pltpu.SMEM),
            row_spec,
            row_spec,
            side_spec,
            pl.BlockSpec((1, span, side_width), lambda lane, flag_ref: (lane, 0, 1)),
            pl.BlockSpec((1, rows, span), lambda lane, flag_ref: (lane, 0, 0)),
        ],
        out_specs=[
            row_spec,
            row_spec,
            pl.BlockSpec(
                (1, rows, 2 * side_width), lambda lane, flag_ref: ((lane + flag_ref[0]) % 2, 0, 0)
            ),
            own_spec,
            own_spec,
            pl.BlockSpec((1, KV_HEADS, GROUP, 128), lambda lane, flag_ref: (lane, 0, 0, 0)),
        ],
    )
    return pl.pallas_call(
        group_kernel,
        grid_spec=grid_spec,
        out_shape=[
            jax.ShapeDtypeStruct((lanes, rows, query_width), jnp.bfloat16),
            jax.ShapeDtypeStruct((lanes, rows, query_width), jnp.bfloat16),
            jax.ShapeDtypeStruct((lanes, rows, 2 * side_width), jnp.bfloat16),
            jax.ShapeDtypeStruct((lanes, rows, side_width), jnp.float32),
            jax.ShapeDtypeStruct((lanes, rows, side_width), jnp.float32),
            jax.ShapeDtypeStruct((lanes, KV_HEADS, GROUP, 128), jnp.float32),
        ],
        cost_estimate=pl.CostEstimate(
            flops=flops, transcendentals=2 * lanes * HEADS * rows * span, bytes_accessed=moved
        ),
    )(flag, sink_logit, queries, out_grad, window, window, allowed)


def per_device(queries, keys, values, doc_bounds, sink_logit, out_grad):
    block_rows = queries.shape[3]
    query_width = queries.shape[4]
    value_width = keys.shape[4]
    pair_count = lax.axis_size("ctx")
    my_index = lax.axis_index("ctx")
    score_scale = 1.0 / math.sqrt(HEAD_DIM)
    at_fold = my_index == pair_count - 1
    last_block = 2 * pair_count - 1
    span = (REACH + 1) * block_rows

    own_pair = jnp.concatenate(
        [keys.reshape(2, block_rows, value_width), values.reshape(2, block_rows, value_width)], axis=2
    )
    prev0, prev1 = neighbour_swap(own_pair[0], own_pair[1], "ctx")
    prev1 = jnp.where(at_fold, own_pair[0], prev1)
    prev_pair = jnp.stack([prev0, prev1])
    window = jnp.concatenate([prev_pair, own_pair], axis=1)

    lane_block = jnp.stack([my_index, last_block - my_index]).astype(jnp.int32)
    row_offsets = jnp.arange(block_rows, dtype=jnp.int32)
    window_offsets = jnp.arange(span, dtype=jnp.int32)
    query_pos = lane_block[:, None] * block_rows + row_offsets[None, :]
    key_pos = (lane_block[:, None] - REACH) * block_rows + window_offsets[None, :]
    first_pos = doc_bounds.reshape(2, 2, block_rows)[:, 0]
    allowed = (key_pos[:, None, :] <= query_pos[:, :, None]) & (
        key_pos[:, None, :] >= first_pos[:, :, None]
    )
    even_flag = (my_index % 2 == 0).astype(jnp.int32)
    attended, dquery, message, key_own, value_own, sink_parts = attend_blocks(
        even_flag.reshape(1),
        sink_logit,
        queries.reshape(2, block_rows, query_width),
        out_grad.reshape(2, block_rows, query_width),
        window,
        allowed.astype(jnp.float32),
    )
    sink_terms = jnp.sum(sink_parts[:, :, :, 0], axis=0)
    sink_grad = all_sum(sink_terms.reshape(HEADS), ("ctx", "dp"))

    is_even = even_flag == 1
    got_first = swap_pairs(message[0], "ctx", 0)
    got_second = swap_pairs(message[1], "ctx", 1)
    into1 = jnp.where(is_even, got_second, got_first)
    into0 = jnp.where(is_even, got_first, got_second)
    into0 = jnp.where(at_fold, message[1], into0)
    arrived = jnp.stack([into0, into1]).astype(jnp.float32)

    out_shape = (1, 1, 2, block_rows, query_width)
    pair_out = (1, 1, 2, block_rows, value_width)
    attn_out = attended.reshape(out_shape)
    query_grad = dquery.reshape(out_shape)
    key_grad = (key_own + arrived[:, :, :value_width]).astype(jnp.bfloat16).reshape(pair_out)
    value_grad = (value_own + arrived[:, :, value_width:]).astype(jnp.bfloat16).reshape(pair_out)
    return (attn_out, query_grad, key_grad, value_grad, sink_grad)


def solution(mesh):
    in_specs = (
        P("dp", "ctx", None, None, None),
        P("dp", "ctx", None, None, None),
        P("dp", "ctx", None, None, None),
        P("dp", "ctx", None, None, None),
        P(),
        P("dp", "ctx", None, None, None),
    )
    out_specs = (
        P("dp", "ctx", None, None, None),
        P("dp", "ctx", None, None, None),
        P("dp", "ctx", None, None, None),
        P("dp", "ctx", None, None, None),
        P(),
    )
    return jax.shard_map(
        per_device, mesh=mesh, in_specs=in_specs, out_specs=out_specs, check_vma=False
    )
```

```python
import math

import jax
import jax.numpy as jnp
from jax import lax
from jax.experimental import pallas as pl
from jax.experimental.pallas import tpu as pltpu
from jax.sharding import PartitionSpec as P

HEADS = 32
KV_HEADS = 4
HEAD_DIM = 128
GROUP = 8
REACH = 1


def shift_up(x, axis):
    size = lax.axis_size(axis)
    return lax.ppermute(x, axis, [(i, i + 1) for i in range(size - 1)])


def shift_down(x, axis):
    size = lax.axis_size(axis)
    return lax.ppermute(x, axis, [(i + 1, i) for i in range(size - 1)])


def swap_pairs(x, axis, offset):
    size = lax.axis_size(axis)
    pairs = []
    for i in range(size):
        partner = i + 1 if (i - offset) % 2 == 0 else i - 1
        if 0 <= partner < size:
            pairs.append((i, partner))
    return lax.ppermute(x, axis, pairs)


def neighbour_swap(to_next, to_prev, axis):
    even = lax.axis_index(axis) % 2 == 0
    first, second = lax.optimization_barrier(
        (jnp.where(even, to_next, to_prev), jnp.where(even, to_prev, to_next))
    )
    got_first = swap_pairs(first, axis, 0)
    got_second = swap_pairs(second, axis, 1)
    from_prev = jnp.where(even, got_second, got_first)
    from_next = jnp.where(even, got_first, got_second)
    return from_prev, from_next


def all_sum(x, axes):
    count = 1
    for axis in axes:
        count *= lax.axis_size(axis)
    spread = jnp.broadcast_to(x[None], (count,) + x.shape)
    return jnp.sum(lax.all_to_all(spread, axes, 0, 0, tiled=True), axis=0)


def group_kernel(
    sink_ref, q_ref, g_ref, k_ref, v_ref, prev0_ref, prev1_ref, allow_ref,
    o_ref, dq_ref, dk_ref, dv_ref, st_ref,
):
    rows = q_ref.shape[1]
    score_scale = 1.0 / math.sqrt(HEAD_DIM)
    contract_last = (((1,), (1,)), ((), ()))
    contract_first = (((0,), (0,)), ((), ()))
    allowed = jnp.concatenate([allow_ref[0]] * GROUP, axis=0) > 0.5
    head_of_row = lax.broadcasted_iota(jnp.int32, (GROUP * rows, 1), 0) // rows
    for group in range(KV_HEADS):
        heads = [pl.ds((group * GROUP + h) * HEAD_DIM, HEAD_DIM) for h in range(GROUP)]
        side = pl.ds(group * HEAD_DIM, HEAD_DIM)
        query = jnp.concatenate([q_ref[0, :, cols] for cols in heads], axis=0)
        grad = jnp.concatenate([g_ref[0, :, cols] for cols in heads], axis=0)
        value_side = pl.ds((KV_HEADS + group) * HEAD_DIM, HEAD_DIM)
        lane_zero = pl.program_id(0) == 0
        prev_key = jnp.where(lane_zero, prev0_ref[:, side], prev1_ref[:, side])
        prev_value = jnp.where(lane_zero, prev0_ref[:, value_side], prev1_ref[:, value_side])
        key = jnp.concatenate([prev_key, k_ref[0, :, side]], axis=0)
        value = jnp.concatenate([prev_value, v_ref[0, :, side]], axis=0)
        sink = jnp.zeros((GROUP * rows, 1), jnp.float32)
        for h in range(GROUP):
            sink = jnp.where(head_of_row == h, sink_ref[group * GROUP + h], sink)
        scores = (
            lax.dot_general(query, key, contract_last, preferred_element_type=jnp.float32)
            * score_scale
        )
        masked = jnp.where(allowed, scores, -jnp.inf)
        row_top = jnp.maximum(sink, jnp.max(masked, axis=1, keepdims=True))
        shifted = jnp.exp(masked - row_top)
        sink_weight = jnp.exp(sink - row_top)
        inverse_total = 1.0 / (sink_weight + jnp.sum(shifted, axis=1, keepdims=True))
        probs = shifted * inverse_total
        weights = probs.astype(jnp.bfloat16)
        attended = jnp.dot(weights, value, preferred_element_type=jnp.float32).astype(
            jnp.bfloat16
        )
        row_delta = jnp.sum(
            grad.astype(jnp.float32) * attended.astype(jnp.float32), axis=1, keepdims=True
        )
        dprob = lax.dot_general(grad, value, contract_last, preferred_element_type=jnp.float32)
        dscore = (probs * (dprob - row_delta)).astype(jnp.bfloat16)
        dquery = jnp.dot(dscore, key, preferred_element_type=jnp.float32) * score_scale
        dk_ref[0, :, side] = (
            lax.dot_general(dscore, query, contract_first, preferred_element_type=jnp.float32)
            * score_scale
        )
        dv_ref[0, :, side] = lax.dot_general(
            weights, grad, contract_first, preferred_element_type=jnp.float32
        )
        sink_share = sink_weight * inverse_total * row_delta
        for h in range(GROUP):
            part = slice(h * rows, (h + 1) * rows)
            o_ref[0, :, heads[h]] = attended[part]
            dq_ref[0, :, heads[h]] = dquery[part].astype(jnp.bfloat16)
            total = -jnp.sum(sink_share[part], axis=0, keepdims=True)
            st_ref[0, group, pl.ds(h, 1), :] = jnp.broadcast_to(total, (1, 128))


def attend_blocks(sink_logit, queries, out_grad, keys, values, prev0, prev1, allowed):
    lanes, rows, query_width = queries.shape
    span = 2 * rows
    side_width = keys.shape[2]
    row_spec = pl.BlockSpec((1, rows, query_width), lambda lane: (lane, 0, 0))
    own_spec = pl.BlockSpec((1, rows, side_width), lambda lane: (lane, 0, 0))
    whole = pl.BlockSpec(prev0.shape, lambda lane: (0, 0))
    side_spec = pl.BlockSpec((1, span, side_width), lambda lane: (lane, 0, 0))
    flops = 2 * lanes * HEADS * rows * span * HEAD_DIM * 6
    moved = 8 * queries.size + 4 * keys.size + 4 * prev0.size + 4 * allowed.size + 16 * keys.size
    return pl.pallas_call(
        group_kernel,
        grid=(lanes,),
        in_specs=[
            pl.BlockSpec(memory_space=pltpu.SMEM),
            row_spec,
            row_spec,
            own_spec,
            own_spec,
            whole,
            whole,
            pl.BlockSpec((1, rows, span), lambda lane: (lane, 0, 0)),
        ],
        out_specs=[
            row_spec,
            row_spec,
            side_spec,
            side_spec,
            pl.BlockSpec((1, KV_HEADS, GROUP, 128), lambda lane: (lane, 0, 0, 0)),
        ],
        out_shape=[
            jax.ShapeDtypeStruct((lanes, rows, query_width), jnp.bfloat16),
            jax.ShapeDtypeStruct((lanes, rows, query_width), jnp.bfloat16),
            jax.ShapeDtypeStruct((lanes, span, side_width), jnp.float32),
            jax.ShapeDtypeStruct((lanes, span, side_width), jnp.float32),
            jax.ShapeDtypeStruct((lanes, KV_HEADS, GROUP, 128), jnp.float32),
        ],
        cost_estimate=pl.CostEstimate(
            flops=flops, transcendentals=2 * lanes * HEADS * rows * span, bytes_accessed=moved
        ),
    )(sink_logit, queries, out_grad, keys, values, prev0, prev1, allowed)


def per_device(queries, keys, values, doc_bounds, sink_logit, out_grad):
    block_rows = queries.shape[3]
    query_width = queries.shape[4]
    value_width = keys.shape[4]
    pair_count = lax.axis_size("ctx")
    my_index = lax.axis_index("ctx")
    score_scale = 1.0 / math.sqrt(HEAD_DIM)
    at_fold = my_index == pair_count - 1
    last_block = 2 * pair_count - 1
    span = (REACH + 1) * block_rows

    own_pair = jnp.concatenate(
        [keys.reshape(2, block_rows, value_width), values.reshape(2, block_rows, value_width)], axis=2
    )
    prev0, prev1 = neighbour_swap(own_pair[0], own_pair[1], "ctx")
    prev1 = jnp.where(at_fold, own_pair[0], prev1)

    lane_block = jnp.stack([my_index, last_block - my_index]).astype(jnp.int32)
    row_offsets = jnp.arange(block_rows, dtype=jnp.int32)
    window_offsets = jnp.arange(span, dtype=jnp.int32)
    query_pos = lane_block[:, None] * block_rows + row_offsets[None, :]
    key_pos = (lane_block[:, None] - REACH) * block_rows + window_offsets[None, :]
    first_pos = doc_bounds.reshape(2, 2, block_rows)[:, 0]
    allowed = (key_pos[:, None, :] <= query_pos[:, :, None]) & (
        key_pos[:, None, :] >= first_pos[:, :, None]
    )
    attended, dquery, key_part, value_part, sink_parts = attend_blocks(
        sink_logit,
        queries.reshape(2, block_rows, query_width),
        out_grad.reshape(2, block_rows, query_width),
        keys.reshape(2, block_rows, value_width),
        values.reshape(2, block_rows, value_width),
        prev0,
        prev1,
        allowed.astype(jnp.float32),
    )
    sink_terms = jnp.sum(sink_parts[:, :, :, 0], axis=0)
    sink_grad = all_sum(sink_terms.reshape(HEADS), ("ctx", "dp"))
    partial = jnp.concatenate([key_part, value_part], axis=2)

    prev_part = partial[:, :block_rows].astype(jnp.bfloat16)
    into1, into0 = neighbour_swap(prev_part[1], prev_part[0], "ctx")
    into0 = jnp.where(at_fold, prev_part[1], into0)
    own_part = partial[:, block_rows:]
    gathered = own_part + jnp.stack([into0, into1]).astype(jnp.float32)

    out_shape = (1, 1, 2, block_rows, query_width)
    pair_out = (1, 1, 2, block_rows, value_width)
    attn_out = attended.reshape(out_shape)
    query_grad = dquery.reshape(out_shape)
    key_grad = gathered[:, :, :value_width].astype(jnp.bfloat16).reshape(pair_out)
    value_grad = gathered[:, :, value_width:].astype(jnp.bfloat16).reshape(pair_out)
    return (attn_out, query_grad, key_grad, value_grad, sink_grad)


def solution(mesh):
    in_specs = (
        P("dp", "ctx", None, None, None),
        P("dp", "ctx", None, None, None),
        P("dp", "ctx", None, None, None),
        P("dp", "ctx", None, None, None),
        P(),
        P("dp", "ctx", None, None, None),
    )
    out_specs = (
        P("dp", "ctx", None, None, None),
        P("dp", "ctx", None, None, None),
        P("dp", "ctx", None, None, None),
        P("dp", "ctx", None, None, None),
        P(),
    )
    return jax.shard_map(
        per_device, mesh=mesh, in_specs=in_specs, out_specs=out_specs, check_vma=False
    )
```
